128 devices in a mesh: dp: 4 (over x_lo, core), expert: 32 (over z, x_hi, y).
Axes of the slice: x: 4 (x_hi: 2, x_lo: 2; x = x_hi * 2 + x_lo), y: 4, z: 4, core: 2. Of those that a mesh axis runs over, the one named last changes fastest.
Arguments:
- tokens_in: bfloat16 [16384, 2048], P(('dp', 'expert')), may hold values from -6 to 6
- out_grad: bfloat16 [16384, 2048], P(('dp', 'expert')), may hold values from -6 to 6
- gate_logits: float32 [16384, 8], P(('dp', 'expert')), may hold values from -6 to 6
- route_ids: int32 [16384, 8], P(('dp', 'expert')), may hold values from 0 to 63, all different within a row; in each aligned block of 128 rows (0 to 127, 128 to 255, ...) at most 18 rows name the same one
- w_gate: bfloat16 [2048, 64, 768], P(None, 'expert'), may hold values from -0.125 to 0.125
- w_up: bfloat16 [2048, 64, 768], P(None, 'expert'), may hold values from -0.125 to 0.125
- w_down: bfloat16 [2048, 64, 768], P(None, 'expert'), may hold values from -0.21875 to 0.21875
Outputs:
- input_grad: bfloat16 [16384, 2048], P(('dp', 'expert'))
- router_grad: float32 [16384, 8], P(('dp', 'expert'))
- weight_grads: bfloat16 [2048, 3, 64, 768], P('dp', None, 'expert')
The draws below stay inside these ranges and needn't reach their ends.
Inputs may be any that keep to these rules, and one draw needn't show every extreme that they name: `route_ids`: the 8 experts of a token differ. In each aligned block of 128 rows (the rows of one device) no expert is named by more than 18 rows, a bound that some block reaches.
All inputs are finite; a program needn't handle non-finite values.
Results may differ from the reference program's by a relative error of at most 0.015.
Values may be sent and summed in bfloat16 or wider, within the bound.
No kernel may reach another device: no remote copies, remote signals or barrier semaphores. Data moves between devices by JAX's collectives and lax.ppermute only.
A program may use at most 192 MiB of HBM per device.

```python
import math
import jax
import jax.numpy as jnp
import numpy as np
from jax import lax

D = 2048
H = 768
TOPK = 8
TOK_DEV = 128
EXPERTS = 64
MOST = 18
TOKENS = 16384
N_DP = 4


def steps_of(key, shape, split, low, high):
    level = 1.0
    for axis_at, shards_of in split:
        draws = jax.random.uniform(jax.random.fold_in(jax.random.fold_in(key, 6), axis_at), (shards_of,), jnp.float32, low / len(split), high / len(split))
        level = level * jnp.repeat(jnp.exp(draws), shape[axis_at] // shards_of).reshape((-1,) + (1,) * (len(shape) - 1 - axis_at))
    return level


def routed_block(key, own, number, rows, count, top, limit, skew):
    order = jax.random.permutation(key, count)
    heavy_load, ordinary = portions_of(count, rows * top, limit, skew, True), portions_of(count, rows * top, limit, skew, False)
    places = jnp.arange(count)

    def named(lengths, rotation):
        used = int((lengths > 0).sum())
        fixed = max(1, used // 4)
        moved = fixed + (places - fixed + rotation * (used - fixed)) % max(1, count - fixed)
        return jnp.zeros((count,), jnp.int32).at[order[jnp.where(places < fixed, places, moved)]].set(jnp.asarray(lengths, jnp.int32))

    lengths = jnp.where(number % 4 == 0, named(heavy_load, number // 4), named(ordinary, number - number // 4 - 1))
    mixed = jax.random.permutation(jax.random.fold_in(own, 3), count)
    source_of, receiver = mixed[0:count // 2 * 2:2], mixed[1:count // 2 * 2:2]
    margin = jnp.minimum(lengths[source_of] - 1, limit - lengths[receiver]) // 2
    margin = jnp.where((source_of == order[0]) | (receiver == order[0]) | (lengths[receiver] == 0), 0, jnp.maximum(margin, 0))
    moved = jax.random.randint(jax.random.fold_in(own, 4), (count // 2,), 0, 1 << 20) % (margin + 1)
    lengths = lengths.at[source_of].add(-moved).at[receiver].add(moved)
    items = jnp.searchsorted(jnp.cumsum(lengths), jnp.arange(rows * top), side="right").astype(jnp.int32)
    grid = items.reshape(top, rows).T
    grid = grid[jax.random.permutation(jax.random.fold_in(own, 1), rows)]
    rotation = jax.random.randint(jax.random.fold_in(own, 2), (rows, 1), 0, top)
    return jnp.take_along_axis(grid, (jnp.arange(top)[None, :] + rotation) % top, axis=1)


def portions_of(number_of, total, bound, slope, full):
    loads = [(1 << 20) // math.isqrt(standing ** slope) + 1 for standing in range(1, number_of + 1)]
    largest = bound if full else min(bound, max(-(-total // number_of), total * loads[0] // sum(loads)))
    least = 1 if total - largest >= number_of - 1 else 0
    holding, spare = [largest] + [least] * (number_of - 1), total - largest - least * (number_of - 1)
    while spare > 0:
        candidates = [i for i in range(1, number_of) if holding[i] < largest] or [i for i in range(1, number_of) if holding[i] < bound]
        pool, left = sum([loads[i] for i in candidates]), spare
        for i in candidates:
            more = min(bound - holding[i], max(1, left * loads[i] // pool), spare)
            holding[i] = holding[i] + more
            spare = spare - more
    return np.array(holding)


def noise(key, shape, width, reach, split=(), held_as=jnp.bfloat16):
    gain = steps_of(key, shape, split, -0.22, 0.18) if split else 1.0
    entries = jax.random.normal(key, shape, jnp.float32) * width * gain
    return jnp.minimum(jnp.maximum(entries, -reach), reach).astype(held_as)


def setup_inputs(seed: int = 0) -> dict:
    streams_of = jax.random.split(jax.random.key(seed), 8)
    tokens_in = noise(streams_of[0], (TOKENS, D), 1.0, 6.0, ((0, 128),))
    out_grad = noise(streams_of[1], (TOKENS, D), 1.0, 6.0, ((0, 128),))
    gate_logits = noise(streams_of[2], (TOKENS, TOPK), 1.5, 6.0, ((0, 128),), jnp.float32)
    route_ids_keys = jax.random.split(jax.random.fold_in(streams_of[3], 1), TOKENS // TOK_DEV)
    route_ids_turns = jax.random.permutation(jax.random.fold_in(streams_of[3], 3), TOKENS // TOK_DEV)
    route_ids = jax.vmap(lambda own, number: routed_block(jax.random.fold_in(streams_of[3], 2), own, number, TOK_DEV, EXPERTS, TOPK, MOST, 2))(route_ids_keys, route_ids_turns).reshape((TOKENS, TOPK))
    w_gate = noise(streams_of[4], (D, EXPERTS, H), D ** -0.5, 0.125, ((1, 32),))
    w_up = noise(streams_of[5], (D, EXPERTS, H), D ** -0.5, 0.125, ((1, 32),))
    w_down = noise(streams_of[6], (D, EXPERTS, H), H ** -0.5, 0.21875, ((1, 32),))
    return dict(tokens_in=tokens_in, out_grad=out_grad, gate_logits=gate_logits, route_ids=route_ids, w_gate=w_gate, w_up=w_up, w_down=w_down)


def combine_weights(gate_logits):
    raised = jnp.exp(gate_logits)
    return raised / lax.optimization_barrier(jnp.sum(raised, axis=1, keepdims=True))

def group_grad(left, right):
    parts = jnp.einsum('gmd,gmh->gdh', left.reshape(N_DP, -1, left.shape[1]).astype(jnp.float32), right.reshape(N_DP, -1, right.shape[1]).astype(jnp.float32), precision=lax.Precision.HIGHEST)
    return parts

def reference(tokens_in, out_grad, gate_logits, route_ids, w_gate, w_up, w_down):
    tok_total = tokens_in.shape[0]
    pair_count = tok_total * TOPK
    block_count = tok_total // TOK_DEV
    weights = combine_weights(gate_logits)
    scaled = (weights[:, :, None] * out_grad[:, None, :].astype(jnp.float32)).astype(jnp.bfloat16)
    scaled = scaled.reshape(pair_count, D)
    flat_ids = route_ids.reshape(-1).astype(jnp.int32)
    block_ids = flat_ids.reshape(block_count, TOK_DEV * TOPK)
    onehot = (block_ids[:, :, None] == jnp.arange(EXPERTS, dtype=jnp.int32)[None, None, :]).astype(jnp.int32)
    before = jnp.cumsum(onehot, axis=1) - onehot
    slot_rank = lax.optimization_barrier(jnp.sum(before * onehot, axis=2)).reshape(-1)
    block_of_pair = jnp.arange(pair_count, dtype=jnp.int32) // (TOK_DEV * TOPK)
    table_pos = flat_ids * (block_count * MOST) + block_of_pair * MOST + slot_rank
    slot_table = jnp.full((EXPERTS * block_count * MOST,), pair_count, jnp.int32)
    slot_table = slot_table.at[table_pos].set(jnp.arange(pair_count, dtype=jnp.int32))
    slot_table = slot_table.reshape(EXPERTS, block_count * MOST)
    zero_row = jnp.zeros((1, D), jnp.bfloat16)
    token_table = jnp.concatenate([tokens_in, zero_row], axis=0)
    scaled_table = jnp.concatenate([scaled, zero_row], axis=0)

    def per_expert(running, inputs):
        rows_grad, probs_all = running
        slot_index, gate_matrix, up_matrix, down_matrix = inputs
        token_index = (slot_index // TOPK).astype(jnp.int32)
        row_tokens = jnp.take(token_table, token_index, axis=0)
        row_scaled = jnp.take(scaled_table, slot_index, axis=0)
        gate_pre = jnp.dot(row_tokens, gate_matrix, preferred_element_type=jnp.float32)
        up_pre = jnp.dot(row_tokens, up_matrix, preferred_element_type=jnp.float32)
        sigmoid_gate = jax.nn.sigmoid(gate_pre)
        active = gate_pre * sigmoid_gate
        hidden = (active * up_pre).astype(jnp.bfloat16)
        hidden_grad = jnp.dot(row_scaled, down_matrix, preferred_element_type=jnp.float32)
        prob_part = lax.optimization_barrier(jnp.sum(hidden_grad * hidden.astype(jnp.float32), axis=1)).astype(jnp.bfloat16)
        gate_grad = (hidden_grad * up_pre * sigmoid_gate * (1.0 + gate_pre * (1.0 - sigmoid_gate))).astype(jnp.bfloat16)
        up_grad = (hidden_grad * active).astype(jnp.bfloat16)
        row_grad = (jnp.dot(gate_grad, gate_matrix.T, preferred_element_type=jnp.float32) + jnp.dot(up_grad, up_matrix.T, preferred_element_type=jnp.float32)).astype(jnp.bfloat16)
        group_parts = jnp.stack([group_grad(row_tokens, gate_grad), group_grad(row_tokens, up_grad), group_grad(row_scaled, hidden)], axis=2)
        rounded_parts = lax.optimization_barrier(group_parts.astype(jnp.bfloat16)).astype(jnp.float32)
        matrix_grads = lax.optimization_barrier(jnp.sum(rounded_parts, axis=0)).astype(jnp.bfloat16)
        rows_grad = rows_grad.at[slot_index].set(row_grad)
        probs_all = probs_all.at[slot_index].set(prob_part)
        return ((rows_grad, probs_all), matrix_grads)
    initial = (jnp.zeros((pair_count + 1, D), jnp.bfloat16), jnp.zeros((pair_count + 1,), jnp.bfloat16))
    matrices = (slot_table, jnp.moveaxis(w_gate, 1, 0), jnp.moveaxis(w_up, 1, 0), jnp.moveaxis(w_down, 1, 0))
    (rows_grad, probs_all), grads = lax.scan(per_expert, initial, matrices)
    input_grad = lax.optimization_barrier(jnp.sum(rows_grad[:pair_count].reshape(tok_total, TOPK, D).astype(jnp.float32), axis=1)).astype(jnp.bfloat16)
    prob_part = probs_all[:pair_count].reshape(tok_total, TOPK).astype(jnp.float32)
    router_grad = prob_part - weights * lax.optimization_barrier(jnp.sum(prob_part, axis=1, keepdims=True))
    weight_grads = jnp.transpose(grads, (1, 2, 0, 3))
    return (input_grad, router_grad, weight_grads)
```

```python
import jax
import jax.numpy as jnp
from jax import lax
from jax.sharding import Mesh
from jax.sharding import PartitionSpec as P


def combine_weights(gate_logits):
    raised = jnp.exp(gate_logits)
    return raised / jnp.sum(raised, axis=1, keepdims=True)


def per_device(tokens_in, out_grad, gate_logits, route_ids, w_gate, w_up, w_down):
    tok_rows, model_width = tokens_in.shape
    topk_count = route_ids.shape[1]
    local_experts = w_gate.shape[1]
    hidden_width = w_gate.shape[2]
    xlo_count = lax.axis_size("xlo")
    core_count = lax.axis_size("core")
    expert_devs = lax.axis_size("expert")
    assert local_experts == xlo_count
    expert_count = local_experts * expert_devs
    dest_count = xlo_count * expert_devs
    capacity = 9 * tok_rows * topk_count // (8 * expert_count)
    pair_count = tok_rows * topk_count
    slot_count = dest_count * capacity
    xlo = lax.axis_index("xlo")
    core = lax.axis_index("core")

    weights = combine_weights(gate_logits)
    flat_ids = route_ids.reshape(-1)
    flat_weights = weights.reshape(-1)

    onehot = (flat_ids[:, None] == jnp.arange(expert_count, dtype=jnp.int32)[None, :]).astype(
        jnp.bfloat16
    )
    pos = jnp.arange(pair_count, dtype=jnp.int32)
    earlier = (pos[None, :] < pos[:, None]).astype(jnp.bfloat16)
    before = jnp.dot(earlier, onehot, preferred_element_type=jnp.float32)
    slot_rank = jnp.sum(before * onehot.astype(jnp.float32), axis=1).astype(jnp.int32)
    dest = (flat_ids % local_experts) * expert_devs + flat_ids // local_experts
    slot_of_pair = dest * capacity + slot_rank

    slot_ids = jnp.arange(slot_count, dtype=jnp.int32)
    pair_hit = slot_of_pair[None, :] == slot_ids[:, None]
    token_hit = jnp.any(pair_hit.reshape(slot_count, tok_rows, topk_count), axis=2)
    dispatch = token_hit.astype(jnp.bfloat16)
    slot_weight = jnp.sum(jnp.where(pair_hit, flat_weights[None, :], 0.0), axis=1)

    send_tokens = jnp.dot(dispatch, tokens_in, preferred_element_type=jnp.float32).astype(
        jnp.bfloat16
    )
    send_grads = jnp.dot(dispatch, out_grad, preferred_element_type=jnp.float32)
    send_scaled = (slot_weight[:, None] * send_grads).astype(jnp.bfloat16)
    send = jnp.concatenate([send_tokens, send_scaled], axis=1).reshape(
        dest_count, capacity, 2 * model_width
    )
    recv = lax.all_to_all(send, ("xlo", "expert"), split_axis=0, concat_axis=0, tiled=True)
    recv = recv.reshape(slot_count, 2 * model_width)
    rows_in = recv[:, :model_width]
    rows_scaled = recv[:, model_width:]

    wg = lax.dynamic_index_in_dim(w_gate, xlo, axis=1, keepdims=False)
    wu = lax.dynamic_index_in_dim(w_up, xlo, axis=1, keepdims=False)
    wd = lax.dynamic_index_in_dim(w_down, xlo, axis=1, keepdims=False)

    gate_pre = jnp.dot(rows_in, wg, preferred_element_type=jnp.float32)
    up_pre = jnp.dot(rows_in, wu, preferred_element_type=jnp.float32)
    sigmoid_gate = jax.nn.sigmoid(gate_pre)
    active = gate_pre * sigmoid_gate
    hidden = (active * up_pre).astype(jnp.bfloat16)
    hidden_grad = jnp.dot(rows_scaled, wd, preferred_element_type=jnp.float32)
    prob_part = jnp.sum(hidden_grad * hidden.astype(jnp.float32), axis=1).astype(jnp.bfloat16)
    gate_grad = (
        hidden_grad * up_pre * sigmoid_gate * (1.0 + gate_pre * (1.0 - sigmoid_gate))
    ).astype(jnp.bfloat16)
    up_grad = (hidden_grad * active).astype(jnp.bfloat16)
    row_grad = (
        jnp.dot(gate_grad, wg.T, preferred_element_type=jnp.float32)
        + jnp.dot(up_grad, wu.T, preferred_element_type=jnp.float32)
    ).astype(jnp.bfloat16)

    back_rows = lax.all_to_all(
        row_grad.reshape(dest_count, capacity, model_width),
        ("xlo", "expert"),
        split_axis=0,
        concat_axis=0,
        tiled=True,
    ).reshape(slot_count, model_width)
    back_probs = lax.all_to_all(
        prob_part.reshape(dest_count, capacity),
        ("xlo", "expert"),
        split_axis=0,
        concat_axis=0,
        tiled=True,
    ).reshape(slot_count)

    input_grad = lax.dot_general(
        dispatch, back_rows, (((0,), (0,)), ((), ())), preferred_element_type=jnp.float32
    ).astype(jnp.bfloat16)
    pair_probs = jnp.sum(
        jnp.where(pair_hit, back_probs.astype(jnp.float32)[:, None], 0.0), axis=0
    ).reshape(tok_rows, topk_count)
    router_grad = pair_probs - weights * jnp.sum(pair_probs, axis=1, keepdims=True)

    contract = (((0,), (0,)), ((), ()))
    grad_gate = lax.dot_general(rows_in, gate_grad, contract, preferred_element_type=jnp.float32)
    grad_up = lax.dot_general(rows_in, up_grad, contract, preferred_element_type=jnp.float32)
    grad_down = lax.dot_general(rows_scaled, hidden, contract, preferred_element_type=jnp.float32)
    block_rows = model_width // (xlo_count * core_count)
    grads = jnp.stack([grad_gate, grad_up, grad_down], axis=1).astype(jnp.bfloat16)
    grads = grads.reshape(xlo_count, core_count, block_rows, 3, hidden_width)

    core_pairs = [(i, (i + 1) % core_count) for i in range(core_count)]
    sibling = lax.dynamic_index_in_dim(grads, 1 - core, axis=1, keepdims=False)
    own = lax.dynamic_index_in_dim(grads, core, axis=1, keepdims=False)
    summed = (
        own.astype(jnp.float32) + lax.ppermute(sibling, "core", core_pairs).astype(jnp.float32)
    ).astype(jnp.bfloat16)

    xlo_pairs = [(i, (i + 1) % xlo_count) for i in range(xlo_count)]
    mine = lax.dynamic_index_in_dim(summed, xlo, axis=0, keepdims=False)
    theirs = lax.ppermute(
        lax.dynamic_index_in_dim(summed, 1 - xlo, axis=0, keepdims=False), "xlo", xlo_pairs
    )
    shares = jnp.where(
        xlo == 0, jnp.stack([mine, theirs], axis=2), jnp.stack([theirs, mine], axis=2)
    )
    return (input_grad, router_grad, shares)


def solution(mesh):
    dp_count, expert_devs = mesh.devices.shape
    core_count = 2
    split_mesh = Mesh(
        mesh.devices.reshape(dp_count // core_count, core_count, expert_devs),
        ("xlo", "core", "expert"),
    )
    rows = ("xlo", "core", "expert")
    in_specs = (
        P(rows, None),
        P(rows, None),
        P(rows, None),
        P(rows, None),
        P(None, "expert", None),
        P(None, "expert", None),
        P(None, "expert", None),
    )
    out_specs = (
        P(rows, None),
        P(rows, None),
        P(("xlo", "core"), None, "expert", None),
    )
    return jax.shard_map(
        per_device, mesh=split_mesh, in_specs=in_specs, out_specs=out_specs, check_vma=False
    )
```

```python
import jax
import jax.numpy as jnp
from jax import lax
from jax.sharding import Mesh
from jax.sharding import PartitionSpec as P


def combine_weights(gate_logits):
    raised = jnp.exp(gate_logits)
    return raised / jnp.sum(raised, axis=1, keepdims=True)


def per_device(tokens_in, out_grad, gate_logits, route_ids, w_gate, w_up, w_down):
    tok_rows, model_width = tokens_in.shape
    topk_count = route_ids.shape[1]
    local_experts = w_gate.shape[1]
    hidden_width = w_gate.shape[2]
    xlo_count = lax.axis_size("xlo")
    core_count = lax.axis_size("core")
    owners = lax.axis_size("expert")
    expert_count = local_experts * owners
    capacity = 9 * tok_rows * topk_count // (8 * expert_count)
    pair_count = tok_rows * topk_count
    slot_count = expert_count * capacity
    xlo = lax.axis_index("xlo")
    core = lax.axis_index("core")

    weights = combine_weights(gate_logits)
    flat_ids = route_ids.reshape(-1)
    flat_weights = weights.reshape(-1)

    onehot = (flat_ids[:, None] == jnp.arange(expert_count, dtype=jnp.int32)[None, :]).astype(
        jnp.bfloat16
    )
    pos = jnp.arange(pair_count, dtype=jnp.int32)
    earlier = (pos[None, :] < pos[:, None]).astype(jnp.bfloat16)
    before = jnp.dot(earlier, onehot, preferred_element_type=jnp.float32)
    slot_rank = jnp.sum(before * onehot.astype(jnp.float32), axis=1).astype(jnp.int32)
    slot_of_pair = flat_ids * capacity + slot_rank

    slot_ids = jnp.arange(slot_count, dtype=jnp.int32)
    pair_hit = slot_of_pair[None, :] == slot_ids[:, None]
    token_hit = jnp.any(pair_hit.reshape(slot_count, tok_rows, topk_count), axis=2)
    dispatch = token_hit.astype(jnp.bfloat16)
    slot_weight = jnp.sum(jnp.where(pair_hit, flat_weights[None, :], 0.0), axis=1)

    send_shape = (owners, local_experts * capacity, model_width)
    send_tokens = jnp.dot(dispatch, tokens_in, preferred_element_type=jnp.float32).astype(
        jnp.bfloat16
    )
    send_grads = jnp.dot(dispatch, out_grad, preferred_element_type=jnp.float32)
    send_scaled = (slot_weight[:, None] * send_grads).astype(jnp.bfloat16)
    recv_tokens = lax.all_to_all(
        send_tokens.reshape(send_shape), "expert", split_axis=0, concat_axis=0, tiled=True
    )
    recv_scaled = lax.all_to_all(
        send_scaled.reshape(send_shape), "expert", split_axis=0, concat_axis=0, tiled=True
    )
    block_shape = (owners, local_experts, capacity, model_width)
    recv_tokens = recv_tokens.reshape(block_shape)
    recv_scaled = recv_scaled.reshape(block_shape)

    gate_pre = jnp.einsum("nemd,deh->nemh", recv_tokens, w_gate, preferred_element_type=jnp.float32)
    up_pre = jnp.einsum("nemd,deh->nemh", recv_tokens, w_up, preferred_element_type=jnp.float32)
    sigmoid_gate = jax.nn.sigmoid(gate_pre)
    active = gate_pre * sigmoid_gate
    hidden = (active * up_pre).astype(jnp.bfloat16)
    hidden_grad = jnp.einsum(
        "nemd,deh->nemh", recv_scaled, w_down, preferred_element_type=jnp.float32
    )
    prob_part = jnp.sum(hidden_grad * hidden.astype(jnp.float32), axis=3).astype(jnp.bfloat16)
    gate_grad = (
        hidden_grad * up_pre * sigmoid_gate * (1.0 + gate_pre * (1.0 - sigmoid_gate))
    ).astype(jnp.bfloat16)
    up_grad = (hidden_grad * active).astype(jnp.bfloat16)
    row_grad = (
        jnp.einsum("nemh,deh->nemd", gate_grad, w_gate, preferred_element_type=jnp.float32)
        + jnp.einsum("nemh,deh->nemd", up_grad, w_up, preferred_element_type=jnp.float32)
    ).astype(jnp.bfloat16)
    back_rows = lax.all_to_all(
        row_grad.reshape(send_shape), "expert", split_axis=0, concat_axis=0, tiled=True
    ).reshape(slot_count, model_width)
    back_probs = lax.all_to_all(
        prob_part.reshape(owners, local_experts * capacity),
        "expert",
        split_axis=0,
        concat_axis=0,
        tiled=True,
    ).reshape(slot_count)

    input_grad = lax.dot_general(
        dispatch, back_rows, (((0,), (0,)), ((), ())), preferred_element_type=jnp.float32
    ).astype(jnp.bfloat16)
    pair_probs = jnp.sum(
        jnp.where(pair_hit, back_probs.astype(jnp.float32)[:, None], 0.0), axis=0
    ).reshape(tok_rows, topk_count)
    router_grad = pair_probs - weights * jnp.sum(pair_probs, axis=1, keepdims=True)

    grad_gate = jnp.einsum(
        "nemd,nemh->deh", recv_tokens, gate_grad, preferred_element_type=jnp.float32
    )
    grad_up = jnp.einsum("nemd,nemh->deh", recv_tokens, up_grad, preferred_element_type=jnp.float32)
    grad_down = jnp.einsum(
        "nemd,nemh->deh", recv_scaled, hidden, preferred_element_type=jnp.float32
    )
    block_rows = model_width // (xlo_count * core_count)
    grads = jnp.stack([grad_gate, grad_up, grad_down], axis=1).astype(jnp.bfloat16)
    grads = grads.reshape(xlo_count, core_count, block_rows, 3, local_experts, hidden_width)

    core_pairs = [(i, (i + 1) % core_count) for i in range(core_count)]
    sibling = lax.dynamic_index_in_dim(grads, 1 - core, axis=1, keepdims=False)
    own = lax.dynamic_index_in_dim(grads, core, axis=1, keepdims=False)
    summed = (
        own.astype(jnp.float32) + lax.ppermute(sibling, "core", core_pairs).astype(jnp.float32)
    ).astype(jnp.bfloat16)

    xlo_pairs = [(i, (i + 1) % xlo_count) for i in range(xlo_count)]
    mine = lax.dynamic_index_in_dim(summed, xlo, axis=0, keepdims=False)
    theirs = lax.ppermute(
        lax.dynamic_index_in_dim(summed, 1 - xlo, axis=0, keepdims=False), "xlo", xlo_pairs
    )
    shares = (mine.astype(jnp.float32) + theirs.astype(jnp.float32)).astype(jnp.bfloat16)
    return (input_grad, router_grad, shares)


def solution(mesh):
    dp_count, expert_devs = mesh.devices.shape
    core_count = 2
    split_mesh = Mesh(
        mesh.devices.reshape(dp_count // core_count, core_count, expert_devs),
        ("xlo", "core", "expert"),
    )
    rows = ("xlo", "core", "expert")
    in_specs = (
        P(rows, None),
        P(rows, None),
        P(rows, None),
        P(rows, None),
        P(None, "expert", None),
        P(None, "expert", None),
        P(None, "expert", None),
    )
    out_specs = (
        P(rows, None),
        P(rows, None),
        P(("xlo", "core"), None, "expert", None),
    )
    return jax.shard_map(
        per_device, mesh=split_mesh, in_specs=in_specs, out_specs=out_specs, check_vma=False
    )
```

```python
import jax
import jax.numpy as jnp
from jax import lax
from jax.sharding import Mesh
from jax.sharding import PartitionSpec as P


def combine_weights(gate_logits):
    raised = jnp.exp(gate_logits)
    return raised / jnp.sum(raised, axis=1, keepdims=True)


def diagonal_groups(xlo_count, owners, hi_stride):
    groups = [[], []]
    for xlo in range(xlo_count):
        for holder in range(owners):
            groups[xlo ^ ((holder // hi_stride) % 2)].append(xlo * owners + holder)
    return groups


def per_device(tokens_in, out_grad, gate_logits, route_ids, w_gate, w_up, w_down):
    tok_rows, model_width = tokens_in.shape
    topk_count = route_ids.shape[1]
    local_experts = w_gate.shape[1]
    hidden_width = w_gate.shape[2]
    xlo_count = lax.axis_size("xlo")
    core_count = lax.axis_size("core")
    owners = lax.axis_size("expert")
    expert_count = local_experts * owners
    capacity = 9 * tok_rows * topk_count // (8 * expert_count)
    pair_count = tok_rows * topk_count
    slot_count = expert_count * capacity
    xlo = lax.axis_index("xlo")
    core = lax.axis_index("core")
    hi_stride = 4
    group_half = owners // 2
    my_xhi = (lax.axis_index("expert") // hi_stride) % 2
    my_group = xlo ^ my_xhi
    groups = diagonal_groups(xlo_count, owners, hi_stride)

    weights = combine_weights(gate_logits)
    flat_ids = route_ids.reshape(-1)
    flat_weights = weights.reshape(-1)

    onehot = (flat_ids[:, None] == jnp.arange(expert_count, dtype=jnp.int32)[None, :]).astype(
        jnp.bfloat16
    )
    pos = jnp.arange(pair_count, dtype=jnp.int32)
    earlier = (pos[None, :] < pos[:, None]).astype(jnp.bfloat16)
    before = jnp.dot(earlier, onehot, preferred_element_type=jnp.float32)
    slot_rank = jnp.sum(before * onehot.astype(jnp.float32), axis=1).astype(jnp.int32)
    holder = flat_ids // local_experts
    holder_xhi = (holder // hi_stride) % 2
    group_pos = (my_group ^ holder_xhi) * group_half + (holder // (2 * hi_stride)) * hi_stride + (
        holder % hi_stride
    )
    slot_of_pair = (group_pos * local_experts + flat_ids % local_experts) * capacity + slot_rank

    slot_ids = jnp.arange(slot_count, dtype=jnp.int32)
    pair_hit = slot_of_pair[None, :] == slot_ids[:, None]
    token_hit = jnp.any(pair_hit.reshape(slot_count, tok_rows, topk_count), axis=2)
    dispatch = token_hit.astype(jnp.bfloat16)
    slot_weight = jnp.sum(jnp.where(pair_hit, flat_weights[None, :], 0.0), axis=1)

    send_shape = (owners, local_experts * capacity, model_width)
    send_tokens = jnp.dot(dispatch, tokens_in, preferred_element_type=jnp.float32).astype(
        jnp.bfloat16
    )
    send_grads = jnp.dot(dispatch, out_grad, preferred_element_type=jnp.float32)
    send_scaled = (slot_weight[:, None] * send_grads).astype(jnp.bfloat16)
    recv_tokens = lax.all_to_all(
        send_tokens.reshape(send_shape), ("xlo", "expert"),
        split_axis=0,
        concat_axis=0,
        tiled=True,
        axis_index_groups=groups,
    )
    recv_scaled = lax.all_to_all(
        send_scaled.reshape(send_shape), ("xlo", "expert"),
        split_axis=0,
        concat_axis=0,
        tiled=True,
        axis_index_groups=groups,
    )
    block_shape = (owners, local_experts, capacity, model_width)
    recv_tokens = recv_tokens.reshape(block_shape)
    recv_scaled = recv_scaled.reshape(block_shape)

    gate_pre = jnp.einsum("nemd,deh->nemh", recv_tokens, w_gate, preferred_element_type=jnp.float32)
    up_pre = jnp.einsum("nemd,deh->nemh", recv_tokens, w_up, preferred_element_type=jnp.float32)
    sigmoid_gate = jax.nn.sigmoid(gate_pre)
    active = gate_pre * sigmoid_gate
    hidden = (active * up_pre).astype(jnp.bfloat16)
    hidden_grad = jnp.einsum(
        "nemd,deh->nemh", recv_scaled, w_down, preferred_element_type=jnp.float32
    )
    prob_part = jnp.sum(hidden_grad * hidden.astype(jnp.float32), axis=3).astype(jnp.bfloat16)
    gate_grad = (
        hidden_grad * up_pre * sigmoid_gate * (1.0 + gate_pre * (1.0 - sigmoid_gate))
    ).astype(jnp.bfloat16)
    up_grad = (hidden_grad * active).astype(jnp.bfloat16)
    row_grad = (
        jnp.einsum("nemh,deh->nemd", gate_grad, w_gate, preferred_element_type=jnp.float32)
        + jnp.einsum("nemh,deh->nemd", up_grad, w_up, preferred_element_type=jnp.float32)
    ).astype(jnp.bfloat16)
    back_rows = lax.all_to_all(
        row_grad.reshape(send_shape), ("xlo", "expert"),
        split_axis=0,
        concat_axis=0,
        tiled=True,
        axis_index_groups=groups,
    ).reshape(slot_count, model_width)
    back_probs = lax.all_to_all(
        prob_part.reshape(owners, local_experts * capacity),
        ("xlo", "expert"),
        split_axis=0,
        concat_axis=0,
        tiled=True,
        axis_index_groups=groups,
    ).reshape(slot_count)

    input_grad = lax.dot_general(
        dispatch, back_rows, (((0,), (0,)), ((), ())), preferred_element_type=jnp.float32
    ).astype(jnp.bfloat16)
    pair_probs = jnp.sum(
        jnp.where(pair_hit, back_probs.astype(jnp.float32)[:, None], 0.0), axis=0
    ).reshape(tok_rows, topk_count)
    router_grad = pair_probs - weights * jnp.sum(pair_probs, axis=1, keepdims=True)

    grad_gate = jnp.einsum(
        "nemd,nemh->deh", recv_tokens, gate_grad, preferred_element_type=jnp.float32
    )
    grad_up = jnp.einsum("nemd,nemh->deh", recv_tokens, up_grad, preferred_element_type=jnp.float32)
    grad_down = jnp.einsum(
        "nemd,nemh->deh", recv_scaled, hidden, preferred_element_type=jnp.float32
    )
    block_rows = model_width // (xlo_count * core_count)
    grads = jnp.stack([grad_gate, grad_up, grad_down], axis=0).astype(jnp.bfloat16)
    grads = grads.reshape(3, xlo_count, core_count, block_rows, local_experts, hidden_width)

    core_pairs = [(i, (i + 1) % core_count) for i in range(core_count)]
    sibling = lax.dynamic_index_in_dim(grads, 1 - core, axis=2, keepdims=False)
    own = lax.dynamic_index_in_dim(grads, core, axis=2, keepdims=False)
    summed = (
        own.astype(jnp.float32) + lax.ppermute(sibling, "core", core_pairs).astype(jnp.float32)
    ).astype(jnp.bfloat16)

    xlo_pairs = [(i, (i + 1) % xlo_count) for i in range(xlo_count)]
    mine = lax.dynamic_index_in_dim(summed, xlo, axis=1, keepdims=False)
    theirs = lax.ppermute(
        lax.dynamic_index_in_dim(summed, 1 - xlo, axis=1, keepdims=False), "xlo", xlo_pairs
    )
    shares = jnp.transpose(
        (mine.astype(jnp.float32) + theirs.astype(jnp.float32)).astype(jnp.bfloat16), (1, 0, 2, 3)
    )
    return (input_grad, router_grad, shares)


def solution(mesh):
    dp_count, expert_devs = mesh.devices.shape
    core_count = 2
    split_mesh = Mesh(
        mesh.devices.reshape(dp_count // core_count, core_count, expert_devs),
        ("xlo", "core", "expert"),
    )
    rows = ("xlo", "core", "expert")
    in_specs = (
        P(rows, None),
        P(rows, None),
        P(rows, None),
        P(rows, None),
        P(None, "expert", None),
        P(None, "expert", None),
        P(None, "expert", None),
    )
    out_specs = (
        P(rows, None),
        P(rows, None),
        P(("xlo", "core"), None, "expert", None),
    )
    return jax.shard_map(
        per_device, mesh=split_mesh, in_specs=in_specs, out_specs=out_specs, check_vma=False
    )
```

```python
import jax
import jax.numpy as jnp
from jax import lax
from jax.sharding import Mesh
from jax.sharding import PartitionSpec as P


def combine_weights(gate_logits):
    raised = jnp.exp(gate_logits)
    return raised / jnp.sum(raised, axis=1, keepdims=True)


def diagonal_groups(xlo_count, owners, hi_stride):
    groups = [[], []]
    for xlo in range(xlo_count):
        for holder in range(owners):
            groups[xlo ^ ((holder // hi_stride) % 2)].append(xlo * owners + holder)
    return groups


def per_device(tokens_in, out_grad, gate_logits, route_ids, w_gate, w_up, w_down):
    tok_rows, model_width = tokens_in.shape
    topk_count = route_ids.shape[1]
    local_experts = w_gate.shape[1]
    hidden_width = w_gate.shape[2]
    xlo_count = lax.axis_size("xlo")
    core_count = lax.axis_size("core")
    owners = lax.axis_size("expert")
    expert_count = local_experts * owners
    capacity = 9 * tok_rows * topk_count // (8 * expert_count)
    pair_count = tok_rows * topk_count
    slot_count = expert_count * capacity
    xlo = lax.axis_index("xlo")
    core = lax.axis_index("core")
    hi_stride = 4
    group_half = owners // 2
    my_xhi = (lax.axis_index("expert") // hi_stride) % 2
    my_group = xlo ^ my_xhi
    groups = diagonal_groups(xlo_count, owners, hi_stride)

    weights = combine_weights(gate_logits)
    flat_ids = route_ids.reshape(-1)
    flat_weights = weights.reshape(-1)

    onehot = (flat_ids[:, None] == jnp.arange(expert_count, dtype=jnp.int32)[None, :]).astype(
        jnp.bfloat16
    )
    pos = jnp.arange(pair_count, dtype=jnp.int32)
    earlier = (pos[None, :] < pos[:, None]).astype(jnp.bfloat16)
    before = jnp.dot(earlier, onehot, preferred_element_type=jnp.float32)
    slot_rank = jnp.sum(before * onehot.astype(jnp.float32), axis=1).astype(jnp.int32)
    holder = flat_ids // local_experts
    holder_xhi = (holder // hi_stride) % 2
    group_pos = (my_group ^ holder_xhi) * group_half + (holder // (2 * hi_stride)) * hi_stride + (
        holder % hi_stride
    )
    slot_of_pair = (group_pos * local_experts + flat_ids % local_experts) * capacity + slot_rank

    slot_ids = jnp.arange(slot_count, dtype=jnp.int32)
    pair_hit = slot_of_pair[None, :] == slot_ids[:, None]
    token_hit = jnp.any(pair_hit.reshape(slot_count, tok_rows, topk_count), axis=2)
    dispatch = token_hit.astype(jnp.bfloat16)
    slot_weight = jnp.sum(jnp.where(pair_hit, flat_weights[None, :], 0.0), axis=1)

    send_shape = (owners, local_experts * capacity, model_width)
    send_tokens = jnp.dot(dispatch, tokens_in, preferred_element_type=jnp.float32).astype(
        jnp.bfloat16
    )
    send_grads = jnp.dot(dispatch, out_grad, preferred_element_type=jnp.float32)
    send_scaled = (slot_weight[:, None] * send_grads).astype(jnp.bfloat16)
    recv_tokens = lax.all_to_all(
        send_tokens.reshape(send_shape), ("xlo", "expert"),
        split_axis=0,
        concat_axis=0,
        tiled=True,
        axis_index_groups=groups,
    )
    recv_scaled = lax.all_to_all(
        send_scaled.reshape(send_shape), ("xlo", "expert"),
        split_axis=0,
        concat_axis=0,
        tiled=True,
        axis_index_groups=groups,
    )
    block_shape = (owners, local_experts, capacity, model_width)
    recv_tokens = recv_tokens.reshape(block_shape)
    recv_scaled = recv_scaled.reshape(block_shape)

    gate_pre = jnp.einsum("nemd,deh->nemh", recv_tokens, w_gate, preferred_element_type=jnp.float32)
    up_pre = jnp.einsum("nemd,deh->nemh", recv_tokens, w_up, preferred_element_type=jnp.float32)
    sigmoid_gate = jax.nn.sigmoid(gate_pre)
    active = gate_pre * sigmoid_gate
    hidden = (active * up_pre).astype(jnp.bfloat16)
    hidden_grad = jnp.einsum(
        "nemd,deh->nemh", recv_scaled, w_down, preferred_element_type=jnp.float32
    )
    prob_part = jnp.sum(hidden_grad * hidden.astype(jnp.float32), axis=3).astype(jnp.bfloat16)
    gate_grad = (
        hidden_grad * up_pre * sigmoid_gate * (1.0 + gate_pre * (1.0 - sigmoid_gate))
    ).astype(jnp.bfloat16)
    up_grad = (hidden_grad * active).astype(jnp.bfloat16)
    row_grad = (
        jnp.einsum("nemh,deh->nemd", gate_grad, w_gate, preferred_element_type=jnp.float32)
        + jnp.einsum("nemh,deh->nemd", up_grad, w_up, preferred_element_type=jnp.float32)
    ).astype(jnp.bfloat16)
    back_rows = lax.all_to_all(
        row_grad.reshape(send_shape), ("xlo", "expert"),
        split_axis=0,
        concat_axis=0,
        tiled=True,
        axis_index_groups=groups,
    ).reshape(slot_count, model_width)
    back_probs = lax.all_to_all(
        prob_part.reshape(owners, local_experts * capacity),
        ("xlo", "expert"),
        split_axis=0,
        concat_axis=0,
        tiled=True,
        axis_index_groups=groups,
    ).reshape(slot_count)

    input_grad = lax.dot_general(
        dispatch, back_rows, (((0,), (0,)), ((), ())), preferred_element_type=jnp.float32
    ).astype(jnp.bfloat16)
    pair_probs = jnp.sum(
        jnp.where(pair_hit, back_probs.astype(jnp.float32)[:, None], 0.0), axis=0
    ).reshape(tok_rows, topk_count)
    router_grad = pair_probs - weights * jnp.sum(pair_probs, axis=1, keepdims=True)

    block_count = xlo_count * core_count
    block_rows = model_width // block_count
    blocks = []
    for block in range(block_count):
        rows = slice(block * block_rows, (block + 1) * block_rows)
        blocks.append(
            jnp.stack(
                [
                    jnp.einsum(
                        "nemh,nemd->ehd",
                        gate_grad,
                        recv_tokens[..., rows],
                        preferred_element_type=jnp.float32,
                    ),
                    jnp.einsum(
                        "nemh,nemd->ehd",
                        up_grad,
                        recv_tokens[..., rows],
                        preferred_element_type=jnp.float32,
                    ),
                    jnp.einsum(
                        "nemh,nemd->ehd",
                        hidden,
                        recv_scaled[..., rows],
                        preferred_element_type=jnp.float32,
                    ),
                ]
            )
        )
    grads = jnp.stack(blocks).astype(jnp.bfloat16)
    grads = grads.reshape((xlo_count, core_count) + grads.shape[1:])

    core_pairs = [(i, (i + 1) % core_count) for i in range(core_count)]
    sibling = lax.dynamic_index_in_dim(grads, 1 - core, axis=1, keepdims=False)
    own = lax.dynamic_index_in_dim(grads, core, axis=1, keepdims=False)
    summed = (
        own.astype(jnp.float32) + lax.ppermute(sibling, "core", core_pairs).astype(jnp.float32)
    ).astype(jnp.bfloat16)

    xlo_pairs = [(i, (i + 1) % xlo_count) for i in range(xlo_count)]
    mine = lax.dynamic_index_in_dim(summed, xlo, axis=0, keepdims=False)
    theirs = lax.ppermute(
        lax.dynamic_index_in_dim(summed, 1 - xlo, axis=0, keepdims=False), "xlo", xlo_pairs
    )
    shares = jnp.transpose(
        (mine.astype(jnp.float32) + theirs.astype(jnp.float32)).astype(jnp.bfloat16), (3, 0, 1, 2)
    )
    return (input_grad, router_grad, shares)


def solution(mesh):
    dp_count, expert_devs = mesh.devices.shape
    core_count = 2
    split_mesh = Mesh(
        mesh.devices.reshape(dp_count // core_count, core_count, expert_devs),
        ("xlo", "core", "expert"),
    )
    rows = ("xlo", "core", "expert")
    in_specs = (
        P(rows, None),
        P(rows, None),
        P(rows, None),
        P(rows, None),
        P(None, "expert", None),
        P(None, "expert", None),
        P(None, "expert", None),
    )
    out_specs = (
        P(rows, None),
        P(rows, None),
        P(("xlo", "core"), None, "expert", None),
    )
    return jax.shard_map(
        per_device, mesh=split_mesh, in_specs=in_specs, out_specs=out_specs, check_vma=False
    )
```

```python
import jax
import jax.numpy as jnp
from jax import lax
from jax.sharding import Mesh
from jax.sharding import PartitionSpec as P


def combine_weights(gate_logits):
    raised = jnp.exp(gate_logits)
    return raised / jnp.sum(raised, axis=1, keepdims=True)


def diagonal_groups(xlo_count, owners, hi_stride):
    groups = [[], []]
    for xlo in range(xlo_count):
        for holder in range(owners):
            groups[xlo ^ ((holder // hi_stride) % 2)].append(xlo * owners + holder)
    return groups


def per_device(tokens_in, out_grad, gate_logits, route_ids, w_gate, w_up, w_down):
    tok_rows, model_width = tokens_in.shape
    topk_count = route_ids.shape[1]
    local_experts = w_gate.shape[1]
    hidden_width = w_gate.shape[2]
    xlo_count = lax.axis_size("xlo")
    core_count = lax.axis_size("core")
    owners = lax.axis_size("expert")
    expert_count = local_experts * owners
    capacity = 9 * tok_rows * topk_count // (8 * expert_count)
    pair_count = tok_rows * topk_count
    slot_count = expert_count * capacity
    xlo = lax.axis_index("xlo")
    core = lax.axis_index("core")
    hi_stride = 4
    group_half = owners // 2
    my_xhi = (lax.axis_index("expert") // hi_stride) % 2
    my_group = xlo ^ my_xhi
    groups = diagonal_groups(xlo_count, owners, hi_stride)

    weights = combine_weights(gate_logits)
    flat_ids = route_ids.reshape(-1)
    flat_weights = weights.reshape(-1)

    onehot = (flat_ids[:, None] == jnp.arange(expert_count, dtype=jnp.int32)[None, :]).astype(
        jnp.bfloat16
    )
    pos = jnp.arange(pair_count, dtype=jnp.int32)
    earlier = (pos[None, :] < pos[:, None]).astype(jnp.bfloat16)
    before = jnp.dot(earlier, onehot, preferred_element_type=jnp.float32)
    slot_rank = jnp.sum(before * onehot.astype(jnp.float32), axis=1).astype(jnp.int32)
    holder = flat_ids // local_experts
    holder_xhi = (holder // hi_stride) % 2
    group_pos = (my_group ^ holder_xhi) * group_half + (holder // (2 * hi_stride)) * hi_stride + (
        holder % hi_stride
    )
    slot_of_pair = (group_pos * local_experts + flat_ids % local_experts) * capacity + slot_rank

    slot_ids = jnp.arange(slot_count, dtype=jnp.int32)
    pair_hit = slot_of_pair[None, :] == slot_ids[:, None]
    token_hit = jnp.any(pair_hit.reshape(slot_count, tok_rows, topk_count), axis=2)
    dispatch = token_hit.astype(jnp.bfloat16)
    slot_weight = jnp.sum(jnp.where(pair_hit, flat_weights[None, :], 0.0), axis=1)

    send_shape = (owners, local_experts * capacity, model_width)
    send_tokens = jnp.dot(dispatch, tokens_in, preferred_element_type=jnp.float32).astype(
        jnp.bfloat16
    )
    send_grads = jnp.dot(dispatch, out_grad, preferred_element_type=jnp.float32)
    send_scaled = (slot_weight[:, None] * send_grads).astype(jnp.bfloat16)
    recv_tokens = lax.all_to_all(
        send_tokens.reshape(send_shape), ("xlo", "expert"),
        split_axis=0,
        concat_axis=0,
        tiled=True,
        axis_index_groups=groups,
    )
    recv_scaled = lax.all_to_all(
        send_scaled.reshape(send_shape), ("xlo", "expert"),
        split_axis=0,
        concat_axis=0,
        tiled=True,
        axis_index_groups=groups,
    )
    block_shape = (owners, local_experts, capacity, model_width)
    recv_tokens = recv_tokens.reshape(block_shape)
    recv_scaled = recv_scaled.reshape(block_shape)

    gate_pre = jnp.einsum("nemd,deh->nemh", recv_tokens, w_gate, preferred_element_type=jnp.float32)
    up_pre = jnp.einsum("nemd,deh->nemh", recv_tokens, w_up, preferred_element_type=jnp.float32)
    sigmoid_gate = jax.nn.sigmoid(gate_pre)
    active = gate_pre * sigmoid_gate
    hidden = (active * up_pre).astype(jnp.bfloat16)
    hidden_grad = jnp.einsum(
        "nemd,deh->nemh", recv_scaled, w_down, preferred_element_type=jnp.float32
    )
    prob_part = jnp.sum(hidden_grad * hidden.astype(jnp.float32), axis=3).astype(jnp.bfloat16)
    gate_grad = (
        hidden_grad * up_pre * sigmoid_gate * (1.0 + gate_pre * (1.0 - sigmoid_gate))
    ).astype(jnp.bfloat16)
    up_grad = (hidden_grad * active).astype(jnp.bfloat16)
    row_grad = (
        jnp.einsum("nemh,deh->nemd", gate_grad, w_gate, preferred_element_type=jnp.float32)
        + jnp.einsum("nemh,deh->nemd", up_grad, w_up, preferred_element_type=jnp.float32)
    ).astype(jnp.bfloat16)
    lane_pad = 128
    prob_cols = jnp.pad(prob_part[..., None], ((0, 0),) * 3 + ((0, lane_pad - 1),))
    back = lax.all_to_all(
        jnp.concatenate([row_grad, prob_cols], axis=3).reshape(
            owners, local_experts * capacity, model_width + lane_pad
        ),
        ("xlo", "expert"),
        split_axis=0,
        concat_axis=0,
        tiled=True,
        axis_index_groups=groups,
    ).reshape(slot_count, model_width + lane_pad)
    back_rows = back[:, :model_width]
    back_probs = back[:, model_width]

    input_grad = lax.dot_general(
        dispatch, back_rows, (((0,), (0,)), ((), ())), preferred_element_type=jnp.float32
    ).astype(jnp.bfloat16)
    pair_probs = jnp.sum(
        jnp.where(pair_hit, back_probs.astype(jnp.float32)[:, None], 0.0), axis=0
    ).reshape(tok_rows, topk_count)
    router_grad = pair_probs - weights * jnp.sum(pair_probs, axis=1, keepdims=True)

    block_count = xlo_count * core_count
    block_rows = model_width // block_count
    blocks = []
    for xlo_side, core_side in ((1, 1), (0, 1), (1, 0), (0, 0)):
        block = (xlo ^ xlo_side) * core_count + (core ^ core_side)
        tokens_rows = lax.dynamic_slice_in_dim(recv_tokens, block * block_rows, block_rows, 3)
        scaled_rows = lax.dynamic_slice_in_dim(recv_scaled, block * block_rows, block_rows, 3)
        blocks.append(
            jnp.stack(
                [
                    jnp.einsum(
                        "nemh,nemd->ehd", gate_grad, tokens_rows, preferred_element_type=jnp.float32
                    ),
                    jnp.einsum(
                        "nemh,nemd->ehd", up_grad, tokens_rows, preferred_element_type=jnp.float32
                    ),
                    jnp.einsum(
                        "nemh,nemd->ehd", hidden, scaled_rows, preferred_element_type=jnp.float32
                    ),
                ]
            ).astype(jnp.bfloat16)
        )

    core_pairs = [(i, (i + 1) % core_count) for i in range(core_count)]
    xlo_pairs = [(i, (i + 1) % xlo_count) for i in range(xlo_count)]
    from_sibling = lax.ppermute(jnp.stack(blocks[:2]), "core", core_pairs)
    summed = (jnp.stack(blocks[2:]).astype(jnp.float32) + from_sibling.astype(jnp.float32)).astype(
        jnp.bfloat16
    )
    theirs = lax.ppermute(summed[0], "xlo", xlo_pairs)
    shares = jnp.transpose(
        (summed[1].astype(jnp.float32) + theirs.astype(jnp.float32)).astype(jnp.bfloat16),
        (3, 0, 1, 2),
    )
    return (input_grad, router_grad, shares)


def solution(mesh):
    dp_count, expert_devs = mesh.devices.shape
    core_count = 2
    split_mesh = Mesh(
        mesh.devices.reshape(dp_count // core_count, core_count, expert_devs),
        ("xlo", "core", "expert"),
    )
    rows = ("xlo", "core", "expert")
    in_specs = (
        P(rows, None),
        P(rows, None),
        P(rows, None),
        P(rows, None),
        P(None, "expert", None),
        P(None, "expert", None),
        P(None, "expert", None),
    )
    out_specs = (
        P(rows, None),
        P(rows, None),
        P(("xlo", "core"), None, "expert", None),
    )
    return jax.shard_map(
        per_device, mesh=split_mesh, in_specs=in_specs, out_specs=out_specs, check_vma=False
    )
```

```python
import jax
import jax.numpy as jnp
from jax import lax
from jax.sharding import Mesh
from jax.sharding import PartitionSpec as P


def combine_weights(gate_logits):
    raised = jnp.exp(gate_logits)
    return raised / jnp.sum(raised, axis=1, keepdims=True)


def diagonal_groups(xlo_count, owners, hi_stride):
    groups = [[], []]
    for xlo in range(xlo_count):
        for holder in range(owners):
            groups[xlo ^ ((holder // hi_stride) % 2)].append(xlo * owners + holder)
    return groups


def per_device(tokens_in, out_grad, gate_logits, route_ids, w_gate, w_up, w_down):
    tok_rows, model_width = tokens_in.shape
    topk_count = route_ids.shape[1]
    local_experts = w_gate.shape[1]
    hidden_width = w_gate.shape[2]
    xlo_count = lax.axis_size("xlo")
    core_count = lax.axis_size("core")
    owners = lax.axis_size("expert")
    expert_count = local_experts * owners
    capacity = 9 * tok_rows * topk_count // (8 * expert_count)
    pair_count = tok_rows * topk_count
    slot_count = expert_count * capacity
    xlo = lax.axis_index("xlo")
    core = lax.axis_index("core")
    hi_stride = 4
    group_half = owners // 2
    my_xhi = (lax.axis_index("expert") // hi_stride) % 2
    my_group = xlo ^ my_xhi
    groups = diagonal_groups(xlo_count, owners, hi_stride)

    weights = combine_weights(gate_logits)
    flat_ids = route_ids.reshape(-1)
    flat_weights = weights.reshape(-1)

    onehot = (flat_ids[:, None] == jnp.arange(expert_count, dtype=jnp.int32)[None, :]).astype(
        jnp.bfloat16
    )
    pos = jnp.arange(pair_count, dtype=jnp.int32)
    earlier = (pos[None, :] < pos[:, None]).astype(jnp.bfloat16)
    before = jnp.dot(earlier, onehot, preferred_element_type=jnp.float32)
    slot_rank = jnp.sum(before * onehot.astype(jnp.float32), axis=1).astype(jnp.int32)
    holder = flat_ids // local_experts
    holder_xhi = (holder // hi_stride) % 2
    group_pos = (my_group ^ holder_xhi) * group_half + (holder // (2 * hi_stride)) * hi_stride + (
        holder % hi_stride
    )
    slot_of_pair = (group_pos * local_experts + flat_ids % local_experts) * capacity + slot_rank

    slot_ids = jnp.arange(slot_count, dtype=jnp.int32)
    pair_hit = slot_of_pair[None, :] == slot_ids[:, None]
    token_hit = jnp.any(pair_hit.reshape(slot_count, tok_rows, topk_count), axis=2)
    dispatch = token_hit.astype(jnp.bfloat16)
    slot_weight = jnp.sum(jnp.where(pair_hit, flat_weights[None, :], 0.0), axis=1)

    send_shape = (owners, local_experts * capacity, 2 * model_width)
    send_tokens = jnp.dot(dispatch, tokens_in, preferred_element_type=jnp.float32).astype(
        jnp.bfloat16
    )
    send_grads = jnp.dot(dispatch, out_grad, preferred_element_type=jnp.float32)
    send_scaled = (slot_weight[:, None] * send_grads).astype(jnp.bfloat16)
    recv = lax.all_to_all(
        jnp.concatenate([send_tokens, send_scaled], axis=1).reshape(send_shape),
        ("xlo", "expert"),
        split_axis=0,
        concat_axis=0,
        tiled=True,
        axis_index_groups=groups,
    )
    recv_tokens = recv[..., :model_width]
    recv_scaled = recv[..., model_width:]
    block_shape = (owners, local_experts, capacity, model_width)
    recv_tokens = recv_tokens.reshape(block_shape)
    recv_scaled = recv_scaled.reshape(block_shape)

    gate_pre = jnp.einsum("nemd,deh->nemh", recv_tokens, w_gate, preferred_element_type=jnp.float32)
    up_pre = jnp.einsum("nemd,deh->nemh", recv_tokens, w_up, preferred_element_type=jnp.float32)
    sigmoid_gate = jax.nn.sigmoid(gate_pre)
    active = gate_pre * sigmoid_gate
    hidden = (active * up_pre).astype(jnp.bfloat16)
    hidden_grad = jnp.einsum(
        "nemd,deh->nemh", recv_scaled, w_down, preferred_element_type=jnp.float32
    )
    prob_part = jnp.sum(hidden_grad * hidden.astype(jnp.float32), axis=3).astype(jnp.bfloat16)
    gate_grad = (
        hidden_grad * up_pre * sigmoid_gate * (1.0 + gate_pre * (1.0 - sigmoid_gate))
    ).astype(jnp.bfloat16)
    up_grad = (hidden_grad * active).astype(jnp.bfloat16)
    row_grad = (
        jnp.einsum("nemh,deh->nemd", gate_grad, w_gate, preferred_element_type=jnp.float32)
        + jnp.einsum("nemh,deh->nemd", up_grad, w_up, preferred_element_type=jnp.float32)
    ).astype(jnp.bfloat16)
    lane_pad = 128
    prob_cols = jnp.pad(prob_part[..., None], ((0, 0),) * 3 + ((0, lane_pad - 1),))
    back = lax.all_to_all(
        jnp.concatenate([row_grad, prob_cols], axis=3).reshape(
            owners, local_experts * capacity, model_width + lane_pad
        ),
        ("xlo", "expert"),
        split_axis=0,
        concat_axis=0,
        tiled=True,
        axis_index_groups=groups,
    ).reshape(slot_count, model_width + lane_pad)
    back_rows = back[:, :model_width]
    back_probs = back[:, model_width]

    input_grad = lax.dot_general(
        dispatch, back_rows, (((0,), (0,)), ((), ())), preferred_element_type=jnp.float32
    ).astype(jnp.bfloat16)
    pair_probs = jnp.sum(
        jnp.where(pair_hit, back_probs.astype(jnp.float32)[:, None], 0.0), axis=0
    ).reshape(tok_rows, topk_count)
    router_grad = pair_probs - weights * jnp.sum(pair_probs, axis=1, keepdims=True)

    block_count = xlo_count * core_count
    block_rows = model_width // block_count
    core_pairs = [(i, (i + 1) % core_count) for i in range(core_count)]
    xlo_pairs = [(i, (i + 1) % xlo_count) for i in range(xlo_count)]
    order = ((1, 1), (0, 1), (1, 0), (0, 0))
    starts = [((xlo ^ a) * core_count + (core ^ c)) * block_rows for a, c in order]
    shares = []
    for left, right in ((gate_grad, recv_tokens), (up_grad, recv_tokens), (hidden, recv_scaled)):
        blocks = [
            jnp.einsum(
                "nemh,nemd->ehd",
                left,
                lax.dynamic_slice_in_dim(right, at, block_rows, 3),
                preferred_element_type=jnp.float32,
            ).astype(jnp.bfloat16)
            for at in starts
        ]
        from_sibling = lax.ppermute(jnp.stack(blocks[:2]), "core", core_pairs)
        summed = (
            jnp.stack(blocks[2:]).astype(jnp.float32) + from_sibling.astype(jnp.float32)
        ).astype(jnp.bfloat16)
        theirs = lax.ppermute(jnp.transpose(summed[0], (2, 0, 1)), "xlo", xlo_pairs)
        mine = jnp.transpose(summed[1], (2, 0, 1))
        shares.append(
            (mine.astype(jnp.float32) + theirs.astype(jnp.float32)).astype(jnp.bfloat16)
        )
    shares = jnp.stack(shares, axis=1)
    return (input_grad, router_grad, shares)


def solution(mesh):
    dp_count, expert_devs = mesh.devices.shape
    core_count = 2
    split_mesh = Mesh(
        mesh.devices.reshape(dp_count // core_count, core_count, expert_devs),
        ("xlo", "core", "expert"),
    )
    rows = ("xlo", "core", "expert")
    in_specs = (
        P(rows, None),
        P(rows, None),
        P(rows, None),
        P(rows, None),
        P(None, "expert", None),
        P(None, "expert", None),
        P(None, "expert", None),
    )
    out_specs = (
        P(rows, None),
        P(rows, None),
        P(("xlo", "core"), None, "expert", None),
    )
    return jax.shard_map(
        per_device, mesh=split_mesh, in_specs=in_specs, out_specs=out_specs, check_vma=False
    )
```

```python
import jax
import jax.numpy as jnp
from jax import lax
from jax.sharding import Mesh
from jax.sharding import PartitionSpec as P


def combine_weights(gate_logits):
    raised = jnp.exp(gate_logits)
    return raised / jnp.sum(raised, axis=1, keepdims=True)


def diagonal_groups(xlo_count, owners, hi_stride):
    groups = [[], []]
    for xlo in range(xlo_count):
        for holder in range(owners):
            groups[xlo ^ ((holder // hi_stride) % 2)].append(xlo * owners + holder)
    return groups


def per_device(tokens_in, out_grad, gate_logits, route_ids, w_gate, w_up, w_down):
    tok_rows, model_width = tokens_in.shape
    topk_count = route_ids.shape[1]
    local_experts = w_gate.shape[1]
    hidden_width = w_gate.shape[2]
    xlo_count = lax.axis_size("xlo")
    core_count = lax.axis_size("core")
    owners = lax.axis_size("expert")
    expert_count = local_experts * owners
    capacity = 9 * tok_rows * topk_count // (8 * expert_count)
    pair_count = tok_rows * topk_count
    slot_count = expert_count * capacity
    xlo = lax.axis_index("xlo")
    core = lax.axis_index("core")
    hi_stride = 4
    group_half = owners // 2
    my_xhi = (lax.axis_index("expert") // hi_stride) % 2
    my_group = xlo ^ my_xhi
    groups = diagonal_groups(xlo_count, owners, hi_stride)

    weights = combine_weights(gate_logits)
    flat_ids = route_ids.reshape(-1)
    flat_weights = weights.reshape(-1)

    onehot = (flat_ids[:, None] == jnp.arange(expert_count, dtype=jnp.int32)[None, :]).astype(
        jnp.bfloat16
    )
    pos = jnp.arange(pair_count, dtype=jnp.int32)
    earlier = (pos[None, :] < pos[:, None]).astype(jnp.bfloat16)
    before = jnp.dot(earlier, onehot, preferred_element_type=jnp.float32)
    slot_rank = jnp.sum(before * onehot.astype(jnp.float32), axis=1).astype(jnp.int32)
    holder = flat_ids // local_experts
    holder_xhi = (holder // hi_stride) % 2
    group_pos = (my_group ^ holder_xhi) * group_half + (holder // (2 * hi_stride)) * hi_stride + (
        holder % hi_stride
    )
    slot_of_pair = (group_pos * local_experts + flat_ids % local_experts) * capacity + slot_rank

    slot_ids = jnp.arange(slot_count, dtype=jnp.int32)
    pair_hit = slot_of_pair[None, :] == slot_ids[:, None]
    token_hit = jnp.any(pair_hit.reshape(slot_count, tok_rows, topk_count), axis=2)
    dispatch = token_hit.astype(jnp.bfloat16)
    slot_weight = jnp.sum(jnp.where(pair_hit, flat_weights[None, :], 0.0), axis=1)

    send_shape = (owners, local_experts * capacity, model_width)
    send_tokens = jnp.dot(dispatch, tokens_in, preferred_element_type=jnp.float32).astype(
        jnp.bfloat16
    )
    send_grads = jnp.dot(dispatch, out_grad, preferred_element_type=jnp.float32)
    send_scaled = (slot_weight[:, None] * send_grads).astype(jnp.bfloat16)
    recv_tokens = lax.all_to_all(
        send_tokens.reshape(send_shape), ("xlo", "expert"),
        split_axis=0,
        concat_axis=0,
        tiled=True,
        axis_index_groups=groups,
    )
    recv_scaled = lax.all_to_all(
        send_scaled.reshape(send_shape), ("xlo", "expert"),
        split_axis=0,
        concat_axis=0,
        tiled=True,
        axis_index_groups=groups,
    )
    block_shape = (owners, local_experts, capacity, model_width)
    recv_tokens = recv_tokens.reshape(block_shape)
    recv_scaled = recv_scaled.reshape(block_shape)

    gate_pre = jnp.einsum("nemd,deh->nemh", recv_tokens, w_gate, preferred_element_type=jnp.float32)
    up_pre = jnp.einsum("nemd,deh->nemh", recv_tokens, w_up, preferred_element_type=jnp.float32)
    sigmoid_gate = jax.nn.sigmoid(gate_pre)
    active = gate_pre * sigmoid_gate
    hidden = (active * up_pre).astype(jnp.bfloat16)
    hidden_grad = jnp.einsum(
        "nemd,deh->nemh", recv_scaled, w_down, preferred_element_type=jnp.float32
    )
    prob_part = jnp.sum(hidden_grad * hidden.astype(jnp.float32), axis=3).astype(jnp.bfloat16)
    gate_grad = (
        hidden_grad * up_pre * sigmoid_gate * (1.0 + gate_pre * (1.0 - sigmoid_gate))
    ).astype(jnp.bfloat16)
    up_grad = (hidden_grad * active).astype(jnp.bfloat16)
    block_count = xlo_count * core_count
    block_rows = model_width // block_count
    blocks = []
    for xlo_side, core_side in ((1, 1), (0, 1), (1, 0), (0, 0)):
        block = (xlo ^ xlo_side) * core_count + (core ^ core_side)
        tokens_rows = lax.dynamic_slice_in_dim(recv_tokens, block * block_rows, block_rows, 3)
        scaled_rows = lax.dynamic_slice_in_dim(recv_scaled, block * block_rows, block_rows, 3)
        blocks.append(
            jnp.stack(
                [
                    jnp.einsum(
                        "nemh,nemd->ehd", gate_grad, tokens_rows, preferred_element_type=jnp.float32
                    ),
                    jnp.einsum(
                        "nemh,nemd->ehd", up_grad, tokens_rows, preferred_element_type=jnp.float32
                    ),
                    jnp.einsum(
                        "nemh,nemd->ehd", hidden, scaled_rows, preferred_element_type=jnp.float32
                    ),
                ]
            ).astype(jnp.bfloat16)
        )

    to_sibling, own_blocks, gate_grad, up_grad = lax.optimization_barrier(
        (jnp.stack(blocks[:2]), jnp.stack(blocks[2:]), gate_grad, up_grad)
    )

    core_pairs = [(i, (i + 1) % core_count) for i in range(core_count)]
    xlo_pairs = [(i, (i + 1) % xlo_count) for i in range(xlo_count)]
    from_sibling = lax.ppermute(to_sibling, "core", core_pairs)
    summed = (own_blocks.astype(jnp.float32) + from_sibling.astype(jnp.float32)).astype(
        jnp.bfloat16
    )
    theirs = lax.ppermute(jnp.transpose(summed[0], (3, 0, 1, 2)), "xlo", xlo_pairs)
    mine = jnp.transpose(summed[1], (3, 0, 1, 2))
    shares = (mine.astype(jnp.float32) + theirs.astype(jnp.float32)).astype(jnp.bfloat16)

    row_grad = (
        jnp.einsum("nemh,deh->nemd", gate_grad, w_gate, preferred_element_type=jnp.float32)
        + jnp.einsum("nemh,deh->nemd", up_grad, w_up, preferred_element_type=jnp.float32)
    ).astype(jnp.bfloat16)
    lane_pad = 128
    prob_cols = jnp.pad(prob_part[..., None], ((0, 0),) * 3 + ((0, lane_pad - 1),))
    back = lax.all_to_all(
        jnp.concatenate([row_grad, prob_cols], axis=3).reshape(
            owners, local_experts * capacity, model_width + lane_pad
        ),
        ("xlo", "expert"),
        split_axis=0,
        concat_axis=0,
        tiled=True,
        axis_index_groups=groups,
    ).reshape(slot_count, model_width + lane_pad)
    back_rows = back[:, :model_width]
    back_probs = back[:, model_width]

    input_grad = lax.dot_general(
        dispatch, back_rows, (((0,), (0,)), ((), ())), preferred_element_type=jnp.float32
    ).astype(jnp.bfloat16)
    pair_probs = jnp.sum(
        jnp.where(pair_hit, back_probs.astype(jnp.float32)[:, None], 0.0), axis=0
    ).reshape(tok_rows, topk_count)
    router_grad = pair_probs - weights * jnp.sum(pair_probs, axis=1, keepdims=True)

    return (input_grad, router_grad, shares)


def solution(mesh):
    dp_count, expert_devs = mesh.devices.shape
    core_count = 2
    split_mesh = Mesh(
        mesh.devices.reshape(dp_count // core_count, core_count, expert_devs),
        ("xlo", "core", "expert"),
    )
    rows = ("xlo", "core", "expert")
    in_specs = (
        P(rows, None),
        P(rows, None),
        P(rows, None),
        P(rows, None),
        P(None, "expert", None),
        P(None, "expert", None),
        P(None, "expert", None),
    )
    out_specs = (
        P(rows, None),
        P(rows, None),
        P(("xlo", "core"), None, "expert", None),
    )
    return jax.shard_map(
        per_device, mesh=split_mesh, in_specs=in_specs, out_specs=out_specs, check_vma=False
    )
```

```python
import jax
import jax.numpy as jnp
from jax import lax
from jax.sharding import Mesh
from jax.sharding import PartitionSpec as P


def combine_weights(gate_logits):
    raised = jnp.exp(gate_logits)
    return raised / jnp.sum(raised, axis=1, keepdims=True)


def diagonal_groups(xlo_count, owners, hi_stride):
    groups = [[], []]
    for xlo in range(xlo_count):
        for holder in range(owners):
            groups[xlo ^ ((holder // hi_stride) % 2)].append(xlo * owners + holder)
    return groups


def per_device(tokens_in, out_grad, gate_logits, route_ids, w_gate, w_up, w_down):
    tok_rows, model_width = tokens_in.shape
    topk_count = route_ids.shape[1]
    local_experts = w_gate.shape[1]
    hidden_width = w_gate.shape[2]
    xlo_count = lax.axis_size("xlo")
    core_count = lax.axis_size("core")
    owners = lax.axis_size("expert")
    expert_count = local_experts * owners
    capacity = 9 * tok_rows * topk_count // (8 * expert_count)
    pair_count = tok_rows * topk_count
    slot_count = expert_count * capacity
    xlo = lax.axis_index("xlo")
    core = lax.axis_index("core")
    hi_stride = 4
    group_half = owners // 2
    my_xhi = (lax.axis_index("expert") // hi_stride) % 2
    my_group = xlo ^ my_xhi
    groups = diagonal_groups(xlo_count, owners, hi_stride)

    weights = combine_weights(gate_logits)
    flat_ids = route_ids.reshape(-1)
    flat_weights = weights.reshape(-1)

    onehot = (flat_ids[:, None] == jnp.arange(expert_count, dtype=jnp.int32)[None, :]).astype(
        jnp.bfloat16
    )
    pos = jnp.arange(pair_count, dtype=jnp.int32)
    earlier = (pos[None, :] < pos[:, None]).astype(jnp.bfloat16)
    before = jnp.dot(earlier, onehot, preferred_element_type=jnp.float32)
    slot_rank = jnp.sum(before * onehot.astype(jnp.float32), axis=1).astype(jnp.int32)
    holder = flat_ids // local_experts
    holder_xhi = (holder // hi_stride) % 2
    group_pos = (my_group ^ holder_xhi) * group_half + (holder // (2 * hi_stride)) * hi_stride + (
        holder % hi_stride
    )
    slot_of_pair = (group_pos * local_experts + flat_ids % local_experts) * capacity + slot_rank

    slot_ids = jnp.arange(slot_count, dtype=jnp.int32)
    pair_hit = slot_of_pair[None, :] == slot_ids[:, None]
    token_hit = jnp.any(pair_hit.reshape(slot_count, tok_rows, topk_count), axis=2)
    dispatch = token_hit.astype(jnp.bfloat16)
    slot_weight = jnp.sum(jnp.where(pair_hit, flat_weights[None, :], 0.0), axis=1)

    send_shape = (owners, local_experts * capacity, model_width)
    send_tokens = jnp.dot(dispatch, tokens_in, preferred_element_type=jnp.float32).astype(
        jnp.bfloat16
    )
    send_grads = jnp.dot(dispatch, out_grad, preferred_element_type=jnp.float32)
    send_scaled = (slot_weight[:, None] * send_grads).astype(jnp.bfloat16)
    recv_tokens = lax.all_to_all(
        send_tokens.reshape(send_shape), ("xlo", "expert"),
        split_axis=0,
        concat_axis=0,
        tiled=True,
        axis_index_groups=groups,
    )
    recv_scaled = lax.all_to_all(
        send_scaled.reshape(send_shape), ("xlo", "expert"),
        split_axis=0,
        concat_axis=0,
        tiled=True,
        axis_index_groups=groups,
    )
    block_shape = (owners, local_experts, capacity, model_width)
    recv_tokens = recv_tokens.reshape(block_shape)
    recv_scaled = recv_scaled.reshape(block_shape)

    gate_pre = jnp.einsum("nemd,deh->nemh", recv_tokens, w_gate, preferred_element_type=jnp.float32)
    up_pre = jnp.einsum("nemd,deh->nemh", recv_tokens, w_up, preferred_element_type=jnp.float32)
    sigmoid_gate = jax.nn.sigmoid(gate_pre)
    active = gate_pre * sigmoid_gate
    hidden = (active * up_pre).astype(jnp.bfloat16)
    hidden_grad = jnp.einsum(
        "nemd,deh->nemh", recv_scaled, w_down, preferred_element_type=jnp.float32
    )
    prob_part = jnp.sum(hidden_grad * hidden.astype(jnp.float32), axis=3).astype(jnp.bfloat16)
    gate_grad = (
        hidden_grad * up_pre * sigmoid_gate * (1.0 + gate_pre * (1.0 - sigmoid_gate))
    ).astype(jnp.bfloat16)
    up_grad = (hidden_grad * active).astype(jnp.bfloat16)
    block_count = xlo_count * core_count
    block_rows = model_width // block_count
    starts = [
        ((xlo ^ xlo_side) * core_count + (core ^ core_side)) * block_rows
        for xlo_side, core_side in ((1, 1), (0, 1), (1, 0), (0, 0))
    ]

    def blocks_of(left, right):
        blocks = [
            jnp.einsum(
                "nemh,nemd->ehd",
                left,
                lax.dynamic_slice_in_dim(right, at, block_rows, 3),
                preferred_element_type=jnp.float32,
            ).astype(jnp.bfloat16)
            for at in starts
        ]
        return jnp.stack(blocks[:2]), jnp.stack(blocks[2:])

    gate_sib, gate_own, up_grad, hidden = lax.optimization_barrier(
        blocks_of(gate_grad, recv_tokens) + (up_grad, hidden)
    )
    up_sib, up_own, hidden = lax.optimization_barrier(
        blocks_of(up_grad, recv_tokens) + (hidden,)
    )
    down_sib, down_own, gate_grad, up_grad = lax.optimization_barrier(
        blocks_of(hidden, recv_scaled) + (gate_grad, up_grad)
    )

    core_pairs = [(i, (i + 1) % core_count) for i in range(core_count)]
    xlo_pairs = [(i, (i + 1) % xlo_count) for i in range(xlo_count)]
    shares = jnp.zeros((block_rows, 3, local_experts, hidden_width), jnp.bfloat16)
    for kind, (sib, own) in enumerate(((gate_sib, gate_own), (up_sib, up_own), (down_sib, down_own))):
        from_sibling = lax.ppermute(sib, "core", core_pairs)
        summed = (own.astype(jnp.float32) + from_sibling.astype(jnp.float32)).astype(jnp.bfloat16)
        theirs = lax.ppermute(summed[0], "xlo", xlo_pairs)
        share = (summed[1].astype(jnp.float32) + theirs.astype(jnp.float32)).astype(jnp.bfloat16)
        shares = lax.dynamic_update_index_in_dim(shares, jnp.transpose(share, (2, 0, 1)), kind, 1)

    row_grad = (
        jnp.einsum("nemh,deh->nemd", gate_grad, w_gate, preferred_element_type=jnp.float32)
        + jnp.einsum("nemh,deh->nemd", up_grad, w_up, preferred_element_type=jnp.float32)
    ).astype(jnp.bfloat16)
    lane_pad = 128
    prob_cols = jnp.pad(prob_part[..., None], ((0, 0),) * 3 + ((0, lane_pad - 1),))
    back = lax.all_to_all(
        jnp.concatenate([row_grad, prob_cols], axis=3).reshape(
            owners, local_experts * capacity, model_width + lane_pad
        ),
        ("xlo", "expert"),
        split_axis=0,
        concat_axis=0,
        tiled=True,
        axis_index_groups=groups,
    ).reshape(slot_count, model_width + lane_pad)
    back_rows = back[:, :model_width]
    back_probs = back[:, model_width]

    input_grad = lax.dot_general(
        dispatch, back_rows, (((0,), (0,)), ((), ())), preferred_element_type=jnp.float32
    ).astype(jnp.bfloat16)
    pair_probs = jnp.sum(
        jnp.where(pair_hit, back_probs.astype(jnp.float32)[:, None], 0.0), axis=0
    ).reshape(tok_rows, topk_count)
    router_grad = pair_probs - weights * jnp.sum(pair_probs, axis=1, keepdims=True)

    return (input_grad, router_grad, shares)


def solution(mesh):
    dp_count, expert_devs = mesh.devices.shape
    core_count = 2
    split_mesh = Mesh(
        mesh.devices.reshape(dp_count // core_count, core_count, expert_devs),
        ("xlo", "core", "expert"),
    )
    rows = ("xlo", "core", "expert")
    in_specs = (
        P(rows, None),
        P(rows, None),
        P(rows, None),
        P(rows, None),
        P(None, "expert", None),
        P(None, "expert", None),
        P(None, "expert", None),
    )
    out_specs = (
        P(rows, None),
        P(rows, None),
        P(("xlo", "core"), None, "expert", None),
    )
    return jax.shard_map(
        per_device, mesh=split_mesh, in_specs=in_specs, out_specs=out_specs, check_vma=False
    )
```

```python
import jax
import jax.numpy as jnp
from jax import lax
from jax.sharding import Mesh
from jax.sharding import PartitionSpec as P


def combine_weights(gate_logits):
    raised = jnp.exp(gate_logits)
    return raised / jnp.sum(raised, axis=1, keepdims=True)


def diagonal_groups(xlo_count, owners, hi_stride):
    groups = [[], []]
    for xlo in range(xlo_count):
        for holder in range(owners):
            groups[xlo ^ ((holder // hi_stride) % 2)].append(xlo * owners + holder)
    return groups


def per_device(tokens_in, out_grad, gate_logits, route_ids, w_gate, w_up, w_down):
    tok_rows, model_width = tokens_in.shape
    topk_count = route_ids.shape[1]
    local_experts = w_gate.shape[1]
    hidden_width = w_gate.shape[2]
    xlo_count = lax.axis_size("xlo")
    core_count = lax.axis_size("core")
    owners = lax.axis_size("expert")
    expert_count = local_experts * owners
    capacity = 9 * tok_rows * topk_count // (8 * expert_count)
    pair_count = tok_rows * topk_count
    slot_count = expert_count * capacity
    xlo = lax.axis_index("xlo")
    core = lax.axis_index("core")
    hi_stride = 4
    group_half = owners // 2
    my_xhi = (lax.axis_index("expert") // hi_stride) % 2
    my_group = xlo ^ my_xhi
    groups = diagonal_groups(xlo_count, owners, hi_stride)

    weights = combine_weights(gate_logits)
    flat_ids = route_ids.reshape(-1)
    flat_weights = weights.reshape(-1)

    onehot = (flat_ids[:, None] == jnp.arange(expert_count, dtype=jnp.int32)[None, :]).astype(
        jnp.bfloat16
    )
    pos = jnp.arange(pair_count, dtype=jnp.int32)
    earlier = (pos[None, :] < pos[:, None]).astype(jnp.bfloat16)
    before = jnp.dot(earlier, onehot, preferred_element_type=jnp.float32)
    slot_rank = jnp.sum(before * onehot.astype(jnp.float32), axis=1).astype(jnp.int32)
    holder = flat_ids // local_experts
    holder_xhi = (holder // hi_stride) % 2
    group_pos = (my_group ^ holder_xhi) * group_half + (holder // (2 * hi_stride)) * hi_stride + (
        holder % hi_stride
    )
    slot_of_pair = (group_pos * local_experts + flat_ids % local_experts) * capacity + slot_rank

    slot_ids = jnp.arange(slot_count, dtype=jnp.int32)
    pair_hit = slot_of_pair[None, :] == slot_ids[:, None]
    token_hit = jnp.any(pair_hit.reshape(slot_count, tok_rows, topk_count), axis=2)
    dispatch = token_hit.astype(jnp.bfloat16)
    slot_weight = jnp.sum(jnp.where(pair_hit, flat_weights[None, :], 0.0), axis=1)

    send_shape = (owners, local_experts * capacity, model_width)
    send_tokens = jnp.dot(dispatch, tokens_in, preferred_element_type=jnp.float32).astype(
        jnp.bfloat16
    )
    send_grads = jnp.dot(dispatch, out_grad, preferred_element_type=jnp.float32)
    send_scaled = (slot_weight[:, None] * send_grads).astype(jnp.bfloat16)
    recv_tokens = lax.all_to_all(
        send_tokens.reshape(send_shape), ("xlo", "expert"),
        split_axis=0,
        concat_axis=0,
        tiled=True,
        axis_index_groups=groups,
    )
    recv_scaled = lax.all_to_all(
        send_scaled.reshape(send_shape), ("xlo", "expert"),
        split_axis=0,
        concat_axis=0,
        tiled=True,
        axis_index_groups=groups,
    )
    block_shape = (owners, local_experts, capacity, model_width)
    recv_tokens = recv_tokens.reshape(block_shape)
    recv_scaled = recv_scaled.reshape(block_shape)

    gate_pre = jnp.einsum("nemd,deh->nemh", recv_tokens, w_gate, preferred_element_type=jnp.float32)
    up_pre = jnp.einsum("nemd,deh->nemh", recv_tokens, w_up, preferred_element_type=jnp.float32)
    sigmoid_gate = jax.nn.sigmoid(gate_pre)
    active = gate_pre * sigmoid_gate
    hidden = (active * up_pre).astype(jnp.bfloat16)
    hidden_grad = jnp.einsum(
        "nemd,deh->nemh", recv_scaled, w_down, preferred_element_type=jnp.float32
    )
    prob_part = jnp.sum(hidden_grad * hidden.astype(jnp.float32), axis=3).astype(jnp.bfloat16)
    gate_grad = (
        hidden_grad * up_pre * sigmoid_gate * (1.0 + gate_pre * (1.0 - sigmoid_gate))
    ).astype(jnp.bfloat16)
    up_grad = (hidden_grad * active).astype(jnp.bfloat16)
    block_count = xlo_count * core_count
    block_rows = model_width // block_count
    starts = [
        ((xlo ^ xlo_side) * core_count + (core ^ core_side)) * block_rows
        for xlo_side, core_side in ((1, 1), (0, 1), (1, 0), (0, 0))
    ]

    def blocks_of(left, right):
        blocks = [
            jnp.einsum(
                "nemh,nemd->ehd",
                left,
                lax.dynamic_slice_in_dim(right, at, block_rows, 3),
                preferred_element_type=jnp.float32,
            ).astype(jnp.bfloat16)
            for at in starts
        ]
        return jnp.stack(blocks[:2]), jnp.stack(blocks[2:])

    core_pairs = [(i, (i + 1) % core_count) for i in range(core_count)]
    xlo_pairs = [(i, (i + 1) % xlo_count) for i in range(xlo_count)]
    gate_sib, gate_own = blocks_of(gate_grad, recv_tokens)
    gate_from, up_grad, hidden = lax.optimization_barrier(
        (lax.ppermute(gate_sib, "core", core_pairs), up_grad, hidden)
    )
    up_sib, up_own = blocks_of(up_grad, recv_tokens)
    up_from, hidden = lax.optimization_barrier((lax.ppermute(up_sib, "core", core_pairs), hidden))
    down_sib, down_own, gate_grad, up_grad = lax.optimization_barrier(
        blocks_of(hidden, recv_scaled) + (gate_grad, up_grad)
    )
    down_from = lax.ppermute(down_sib, "core", core_pairs)

    shares = jnp.zeros((block_rows, 3, local_experts, hidden_width), jnp.bfloat16)
    pieces = ((gate_from, gate_own), (up_from, up_own), (down_from, down_own))
    for kind, (from_sibling, own) in enumerate(pieces):
        summed = (own.astype(jnp.float32) + from_sibling.astype(jnp.float32)).astype(jnp.bfloat16)
        theirs = lax.ppermute(summed[0], "xlo", xlo_pairs)
        share = (summed[1].astype(jnp.float32) + theirs.astype(jnp.float32)).astype(jnp.bfloat16)
        shares = lax.dynamic_update_index_in_dim(shares, jnp.transpose(share, (2, 0, 1)), kind, 1)

    row_grad = (
        jnp.einsum("nemh,deh->nemd", gate_grad, w_gate, preferred_element_type=jnp.float32)
        + jnp.einsum("nemh,deh->nemd", up_grad, w_up, preferred_element_type=jnp.float32)
    ).astype(jnp.bfloat16)
    lane_pad = 128
    prob_cols = jnp.pad(prob_part[..., None], ((0, 0),) * 3 + ((0, lane_pad - 1),))
    back = lax.all_to_all(
        jnp.concatenate([row_grad, prob_cols], axis=3).reshape(
            owners, local_experts * capacity, model_width + lane_pad
        ),
        ("xlo", "expert"),
        split_axis=0,
        concat_axis=0,
        tiled=True,
        axis_index_groups=groups,
    ).reshape(slot_count, model_width + lane_pad)
    back_rows = back[:, :model_width]
    back_probs = back[:, model_width]

    input_grad = lax.dot_general(
        dispatch, back_rows, (((0,), (0,)), ((), ())), preferred_element_type=jnp.float32
    ).astype(jnp.bfloat16)
    pair_probs = jnp.sum(
        jnp.where(pair_hit, back_probs.astype(jnp.float32)[:, None], 0.0), axis=0
    ).reshape(tok_rows, topk_count)
    router_grad = pair_probs - weights * jnp.sum(pair_probs, axis=1, keepdims=True)

    return (input_grad, router_grad, shares)


def solution(mesh):
    dp_count, expert_devs = mesh.devices.shape
    core_count = 2
    split_mesh = Mesh(
        mesh.devices.reshape(dp_count // core_count, core_count, expert_devs),
        ("xlo", "core", "expert"),
    )
    rows = ("xlo", "core", "expert")
    in_specs = (
        P(rows, None),
        P(rows, None),
        P(rows, None),
        P(rows, None),
        P(None, "expert", None),
        P(None, "expert", None),
        P(None, "expert", None),
    )
    out_specs = (
        P(rows, None),
        P(rows, None),
        P(("xlo", "core"), None, "expert", None),
    )
    return jax.shard_map(
        per_device, mesh=split_mesh, in_specs=in_specs, out_specs=out_specs, check_vma=False
    )
```

```python
import jax
import jax.numpy as jnp
from jax import lax
from jax.sharding import Mesh
from jax.sharding import PartitionSpec as P


def combine_weights(gate_logits):
    raised = jnp.exp(gate_logits)
    return raised / jnp.sum(raised, axis=1, keepdims=True)


def diagonal_groups(xlo_count, owners, hi_stride):
    groups = [[], []]
    for xlo in range(xlo_count):
        for holder in range(owners):
            groups[xlo ^ ((holder // hi_stride) % 2)].append(xlo * owners + holder)
    return groups


def per_device(tokens_in, out_grad, gate_logits, route_ids, w_gate, w_up, w_down):
    tok_rows, model_width = tokens_in.shape
    topk_count = route_ids.shape[1]
    local_experts = w_gate.shape[1]
    hidden_width = w_gate.shape[2]
    xlo_count = lax.axis_size("xlo")
    core_count = lax.axis_size("core")
    owners = lax.axis_size("expert")
    expert_count = local_experts * owners
    capacity = 9 * tok_rows * topk_count // (8 * expert_count)
    pair_count = tok_rows * topk_count
    slot_count = expert_count * capacity
    xlo = lax.axis_index("xlo")
    core = lax.axis_index("core")
    hi_stride = 4
    group_half = owners // 2
    my_xhi = (lax.axis_index("expert") // hi_stride) % 2
    my_group = xlo ^ my_xhi
    groups = diagonal_groups(xlo_count, owners, hi_stride)

    weights = combine_weights(gate_logits)
    flat_ids = route_ids.reshape(-1)
    flat_weights = weights.reshape(-1)

    onehot = (flat_ids[:, None] == jnp.arange(expert_count, dtype=jnp.int32)[None, :]).astype(
        jnp.bfloat16
    )
    pos = jnp.arange(pair_count, dtype=jnp.int32)
    earlier = (pos[None, :] < pos[:, None]).astype(jnp.bfloat16)
    before = jnp.dot(earlier, onehot, preferred_element_type=jnp.float32)
    slot_rank = jnp.sum(before * onehot.astype(jnp.float32), axis=1).astype(jnp.int32)
    holder = flat_ids // local_experts
    holder_xhi = (holder // hi_stride) % 2
    group_pos = (my_group ^ holder_xhi) * group_half + (holder // (2 * hi_stride)) * hi_stride + (
        holder % hi_stride
    )
    slot_of_pair = (group_pos * local_experts + flat_ids % local_experts) * capacity + slot_rank

    slot_ids = jnp.arange(slot_count, dtype=jnp.int32)
    pair_hit = slot_of_pair[None, :] == slot_ids[:, None]
    token_hit = jnp.any(pair_hit.reshape(slot_count, tok_rows, topk_count), axis=2)
    dispatch = token_hit.astype(jnp.bfloat16)
    slot_weight = jnp.sum(jnp.where(pair_hit, flat_weights[None, :], 0.0), axis=1)

    block_count = xlo_count * core_count
    block_rows = model_width // block_count
    starts = [
        ((xlo ^ xlo_side) * core_count + (core ^ core_side)) * block_rows
        for xlo_side, core_side in ((1, 1), (0, 1), (1, 0), (0, 0))
    ]
    core_pairs = [(i, (i + 1) % core_count) for i in range(core_count)]
    xlo_pairs = [(i, (i + 1) % xlo_count) for i in range(xlo_count)]
    lane_pad = 128
    expert_slots = owners * capacity
    dispatch = dispatch.reshape(owners, local_experts, capacity, tok_rows)
    slot_weight = slot_weight.reshape(owners, local_experts, capacity)
    pair_hit = pair_hit.reshape(owners, local_experts, capacity, pair_count)

    shares = jnp.zeros((block_rows, 3, local_experts, hidden_width), jnp.bfloat16)
    combined = jnp.zeros((tok_rows, model_width), jnp.float32)
    pair_probs = jnp.zeros((pair_count,), jnp.float32)
    for local in range(local_experts):
        picks = dispatch[:, local].reshape(expert_slots, tok_rows)
        send_tokens = jnp.dot(picks, tokens_in, preferred_element_type=jnp.float32)
        send_grads = jnp.dot(picks, out_grad, preferred_element_type=jnp.float32)
        send_scaled = slot_weight[:, local].reshape(expert_slots, 1) * send_grads
        send = jnp.concatenate([send_tokens, send_scaled], axis=1).astype(jnp.bfloat16)
        recv = lax.all_to_all(
            send.reshape(owners, capacity, 2 * model_width),
            ("xlo", "expert"),
            split_axis=0,
            concat_axis=0,
            tiled=True,
            axis_index_groups=groups,
        ).reshape(expert_slots, 2 * model_width)
        rows_in = recv[:, :model_width]
        rows_scaled = recv[:, model_width:]
        wg = w_gate[:, local]
        wu = w_up[:, local]
        wd = w_down[:, local]

        gate_pre = jnp.dot(rows_in, wg, preferred_element_type=jnp.float32)
        up_pre = jnp.dot(rows_in, wu, preferred_element_type=jnp.float32)
        sigmoid_gate = jax.nn.sigmoid(gate_pre)
        active = gate_pre * sigmoid_gate
        hidden = (active * up_pre).astype(jnp.bfloat16)
        hidden_grad = jnp.dot(rows_scaled, wd, preferred_element_type=jnp.float32)
        prob_part = jnp.sum(hidden_grad * hidden.astype(jnp.float32), axis=1).astype(
            jnp.bfloat16
        )
        gate_grad = (
            hidden_grad * up_pre * sigmoid_gate * (1.0 + gate_pre * (1.0 - sigmoid_gate))
        ).astype(jnp.bfloat16)
        up_grad = (hidden_grad * active).astype(jnp.bfloat16)

        blocks = [
            jnp.stack(
                [
                    lax.dot_general(
                        left,
                        lax.dynamic_slice_in_dim(right, at, block_rows, 1),
                        (((0,), (0,)), ((), ())),
                        preferred_element_type=jnp.float32,
                    )
                    for left, right in (
                        (gate_grad, rows_in),
                        (up_grad, rows_in),
                        (hidden, rows_scaled),
                    )
                ]
            ).astype(jnp.bfloat16)
            for at in starts
        ]
        to_sibling, own_blocks, gate_grad, up_grad = lax.optimization_barrier(
            (jnp.stack(blocks[:2]), jnp.stack(blocks[2:]), gate_grad, up_grad)
        )
        from_sibling = lax.ppermute(to_sibling, "core", core_pairs)
        summed = (own_blocks.astype(jnp.float32) + from_sibling.astype(jnp.float32)).astype(
            jnp.bfloat16
        )
        theirs = lax.ppermute(summed[0], "xlo", xlo_pairs)
        share = (summed[1].astype(jnp.float32) + theirs.astype(jnp.float32)).astype(jnp.bfloat16)
        shares = lax.dynamic_update_index_in_dim(
            shares, jnp.transpose(share, (2, 0, 1)), local, 2
        )

        row_grad = (
            jnp.dot(gate_grad, wg.T, preferred_element_type=jnp.float32)
            + jnp.dot(up_grad, wu.T, preferred_element_type=jnp.float32)
        ).astype(jnp.bfloat16)
        prob_cols = jnp.pad(prob_part[:, None], ((0, 0), (0, lane_pad - 1)))
        back = lax.all_to_all(
            jnp.concatenate([row_grad, prob_cols], axis=1).reshape(
                owners, capacity, model_width + lane_pad
            ),
            ("xlo", "expert"),
            split_axis=0,
            concat_axis=0,
            tiled=True,
            axis_index_groups=groups,
        ).reshape(expert_slots, model_width + lane_pad)
        combined = combined + lax.dot_general(
            picks, back[:, :model_width], (((0,), (0,)), ((), ())),
            preferred_element_type=jnp.float32,
        )
        hits = pair_hit[:, local].reshape(expert_slots, pair_count)
        pair_probs = pair_probs + jnp.sum(
            jnp.where(hits, back[:, model_width].astype(jnp.float32)[:, None], 0.0), axis=0
        )

    input_grad = combined.astype(jnp.bfloat16)
    pair_probs = pair_probs.reshape(tok_rows, topk_count)
    router_grad = pair_probs - weights * jnp.sum(pair_probs, axis=1, keepdims=True)

    return (input_grad, router_grad, shares)


def solution(mesh):
    dp_count, expert_devs = mesh.devices.shape
    core_count = 2
    split_mesh = Mesh(
        mesh.devices.reshape(dp_count // core_count, core_count, expert_devs),
        ("xlo", "core", "expert"),
    )
    rows = ("xlo", "core", "expert")
    in_specs = (
        P(rows, None),
        P(rows, None),
        P(rows, None),
        P(rows, None),
        P(None, "expert", None),
        P(None, "expert", None),
        P(None, "expert", None),
    )
    out_specs = (
        P(rows, None),
        P(rows, None),
        P(("xlo", "core"), None, "expert", None),
    )
    return jax.shard_map(
        per_device, mesh=split_mesh, in_specs=in_specs, out_specs=out_specs, check_vma=False
    )
```

```python
import jax
import jax.numpy as jnp
from jax import lax
from jax.experimental.layout import Layout, with_layout_constraint
from jax.sharding import Mesh
from jax.sharding import PartitionSpec as P


def combine_weights(gate_logits):
    raised = jnp.exp(gate_logits)
    return raised / jnp.sum(raised, axis=1, keepdims=True)


def diagonal_groups(xlo_count, owners, hi_stride):
    groups = [[], []]
    for xlo in range(xlo_count):
        for holder in range(owners):
            groups[xlo ^ ((holder // hi_stride) % 2)].append(xlo * owners + holder)
    return groups


def per_device(tokens_in, out_grad, gate_logits, route_ids, w_gate, w_up, w_down):
    tok_rows, model_width = tokens_in.shape
    topk_count = route_ids.shape[1]
    local_experts = w_gate.shape[1]
    hidden_width = w_gate.shape[2]
    xlo_count = lax.axis_size("xlo")
    core_count = lax.axis_size("core")
    owners = lax.axis_size("expert")
    expert_count = local_experts * owners
    capacity = 9 * tok_rows * topk_count // (8 * expert_count)
    pair_count = tok_rows * topk_count
    slot_count = expert_count * capacity
    xlo = lax.axis_index("xlo")
    core = lax.axis_index("core")
    hi_stride = 4
    group_half = owners // 2
    my_xhi = (lax.axis_index("expert") // hi_stride) % 2
    my_group = xlo ^ my_xhi
    groups = diagonal_groups(xlo_count, owners, hi_stride)

    weights = combine_weights(gate_logits)
    flat_ids = route_ids.reshape(-1)
    flat_weights = weights.reshape(-1)

    onehot = (flat_ids[:, None] == jnp.arange(expert_count, dtype=jnp.int32)[None, :]).astype(
        jnp.bfloat16
    )
    pos = jnp.arange(pair_count, dtype=jnp.int32)
    earlier = (pos[None, :] < pos[:, None]).astype(jnp.bfloat16)
    before = jnp.dot(earlier, onehot, preferred_element_type=jnp.float32)
    slot_rank = jnp.sum(before * onehot.astype(jnp.float32), axis=1).astype(jnp.int32)
    holder = flat_ids // local_experts
    holder_xhi = (holder // hi_stride) % 2
    group_pos = (my_group ^ holder_xhi) * group_half + (holder // (2 * hi_stride)) * hi_stride + (
        holder % hi_stride
    )
    slot_of_pair = (group_pos * local_experts + flat_ids % local_experts) * capacity + slot_rank

    slot_ids = jnp.arange(slot_count, dtype=jnp.int32)
    pair_hit = slot_of_pair[None, :] == slot_ids[:, None]
    token_hit = jnp.any(pair_hit.reshape(slot_count, tok_rows, topk_count), axis=2)
    dispatch = token_hit.astype(jnp.bfloat16)
    slot_weight = jnp.sum(jnp.where(pair_hit, flat_weights[None, :], 0.0), axis=1)

    send_shape = (owners, local_experts * capacity, model_width)
    send_tokens = jnp.dot(dispatch, tokens_in, preferred_element_type=jnp.float32).astype(
        jnp.bfloat16
    )
    send_grads = jnp.dot(dispatch, out_grad, preferred_element_type=jnp.float32)
    send_scaled = (slot_weight[:, None] * send_grads).astype(jnp.bfloat16)
    recv_tokens = lax.all_to_all(
        send_tokens.reshape(send_shape), ("xlo", "expert"),
        split_axis=0,
        concat_axis=0,
        tiled=True,
        axis_index_groups=groups,
    )
    recv_scaled = lax.all_to_all(
        send_scaled.reshape(send_shape), ("xlo", "expert"),
        split_axis=0,
        concat_axis=0,
        tiled=True,
        axis_index_groups=groups,
    )
    block_shape = (owners, local_experts, capacity, model_width)
    recv_tokens = recv_tokens.reshape(block_shape)
    recv_scaled = recv_scaled.reshape(block_shape)

    gate_pre = jnp.einsum("nemd,deh->nemh", recv_tokens, w_gate, preferred_element_type=jnp.float32)
    up_pre = jnp.einsum("nemd,deh->nemh", recv_tokens, w_up, preferred_element_type=jnp.float32)
    sigmoid_gate = jax.nn.sigmoid(gate_pre)
    active = gate_pre * sigmoid_gate
    hidden = (active * up_pre).astype(jnp.bfloat16)
    hidden_grad = jnp.einsum(
        "nemd,deh->nemh", recv_scaled, w_down, preferred_element_type=jnp.float32
    )
    prob_part = jnp.sum(hidden_grad * hidden.astype(jnp.float32), axis=3).astype(jnp.bfloat16)
    gate_grad = (
        hidden_grad * up_pre * sigmoid_gate * (1.0 + gate_pre * (1.0 - sigmoid_gate))
    ).astype(jnp.bfloat16)
    up_grad = (hidden_grad * active).astype(jnp.bfloat16)
    block_count = xlo_count * core_count
    block_rows = model_width // block_count
    starts = [
        ((xlo ^ xlo_side) * core_count + (core ^ core_side)) * block_rows
        for xlo_side, core_side in ((1, 1), (0, 1), (1, 0), (0, 0))
    ]

    def blocks_of(left, right):
        blocks = [
            jnp.einsum(
                "nemh,nemd->ehd",
                left,
                lax.dynamic_slice_in_dim(right, at, block_rows, 3),
                preferred_element_type=jnp.float32,
            ).astype(jnp.bfloat16)
            for at in starts
        ]
        return jnp.stack(blocks[:2]), jnp.stack(blocks[2:])

    core_pairs = [(i, (i + 1) % core_count) for i in range(core_count)]
    xlo_pairs = [(i, (i + 1) % xlo_count) for i in range(xlo_count)]
    gate_sib, gate_own = blocks_of(gate_grad, recv_tokens)
    gate_from, up_grad, hidden = lax.optimization_barrier(
        (lax.ppermute(gate_sib, "core", core_pairs), up_grad, hidden)
    )
    up_sib, up_own = blocks_of(up_grad, recv_tokens)
    up_from, hidden = lax.optimization_barrier((lax.ppermute(up_sib, "core", core_pairs), hidden))
    down_sib, down_own, gate_grad, up_grad = lax.optimization_barrier(
        blocks_of(hidden, recv_scaled) + (gate_grad, up_grad)
    )
    down_from = lax.ppermute(down_sib, "core", core_pairs)

    shares = []
    pieces = ((gate_from, gate_own), (up_from, up_own), (down_from, down_own))
    for kind, (from_sibling, own) in enumerate(pieces):
        summed = (own.astype(jnp.float32) + from_sibling.astype(jnp.float32)).astype(jnp.bfloat16)
        theirs = lax.ppermute(summed[0], "xlo", xlo_pairs)
        share = (summed[1].astype(jnp.float32) + theirs.astype(jnp.float32)).astype(jnp.bfloat16)
        shares.append(with_layout_constraint(jnp.transpose(share, (2, 0, 1)), Layout((0, 1, 2))))

    shares = with_layout_constraint(jnp.stack(shares, axis=1), Layout((0, 1, 2, 3)))
    row_grad = (
        jnp.einsum("nemh,deh->nemd", gate_grad, w_gate, preferred_element_type=jnp.float32)
        + jnp.einsum("nemh,deh->nemd", up_grad, w_up, preferred_element_type=jnp.float32)
    ).astype(jnp.bfloat16)
    lane_pad = 128
    prob_cols = jnp.pad(prob_part[..., None], ((0, 0),) * 3 + ((0, lane_pad - 1),))
    back = lax.all_to_all(
        jnp.concatenate([row_grad, prob_cols], axis=3).reshape(
            owners, local_experts * capacity, model_width + lane_pad
        ),
        ("xlo", "expert"),
        split_axis=0,
        concat_axis=0,
        tiled=True,
        axis_index_groups=groups,
    ).reshape(slot_count, model_width + lane_pad)
    back_rows = back[:, :model_width]
    back_probs = back[:, model_width]

    input_grad = lax.dot_general(
        dispatch, back_rows, (((0,), (0,)), ((), ())), preferred_element_type=jnp.float32
    ).astype(jnp.bfloat16)
    pair_probs = jnp.sum(
        jnp.where(pair_hit, back_probs.astype(jnp.float32)[:, None], 0.0), axis=0
    ).reshape(tok_rows, topk_count)
    router_grad = pair_probs - weights * jnp.sum(pair_probs, axis=1, keepdims=True)

    return (input_grad, router_grad, shares)


def solution(mesh):
    dp_count, expert_devs = mesh.devices.shape
    core_count = 2
    split_mesh = Mesh(
        mesh.devices.reshape(dp_count // core_count, core_count, expert_devs),
        ("xlo", "core", "expert"),
    )
    rows = ("xlo", "core", "expert")
    in_specs = (
        P(rows, None),
        P(rows, None),
        P(rows, None),
        P(rows, None),
        P(None, "expert", None),
        P(None, "expert", None),
        P(None, "expert", None),
    )
    out_specs = (
        P(rows, None),
        P(rows, None),
        P(("xlo", "core"), None, "expert", None),
    )
    return jax.shard_map(
        per_device, mesh=split_mesh, in_specs=in_specs, out_specs=out_specs, check_vma=False
    )
```

```python
import jax
import jax.numpy as jnp
from jax import lax
from jax.sharding import Mesh
from jax.sharding import PartitionSpec as P


def combine_weights(gate_logits):
    raised = jnp.exp(gate_logits)
    return raised / jnp.sum(raised, axis=1, keepdims=True)


def diagonal_groups(xlo_count, owners, hi_stride):
    groups = [[], []]
    for xlo in range(xlo_count):
        for holder in range(owners):
            groups[xlo ^ ((holder // hi_stride) % 2)].append(xlo * owners + holder)
    return groups


def per_device(tokens_in, out_grad, gate_logits, route_ids, w_gate, w_up, w_down):
    tok_rows, model_width = tokens_in.shape
    topk_count = route_ids.shape[1]
    local_experts = w_gate.shape[1]
    hidden_width = w_gate.shape[2]
    xlo_count = lax.axis_size("xlo")
    core_count = lax.axis_size("core")
    owners = lax.axis_size("expert")
    expert_count = local_experts * owners
    capacity = 9 * tok_rows * topk_count // (8 * expert_count)
    pair_count = tok_rows * topk_count
    slot_count = expert_count * capacity
    xlo = lax.axis_index("xlo")
    core = lax.axis_index("core")
    hi_stride = 4
    group_half = owners // 2
    my_xhi = (lax.axis_index("expert") // hi_stride) % 2
    my_group = xlo ^ my_xhi
    groups = diagonal_groups(xlo_count, owners, hi_stride)

    weights = combine_weights(gate_logits)
    flat_ids = route_ids.reshape(-1)
    flat_weights = weights.reshape(-1)

    onehot = (flat_ids[:, None] == jnp.arange(expert_count, dtype=jnp.int32)[None, :]).astype(
        jnp.bfloat16
    )
    pos = jnp.arange(pair_count, dtype=jnp.int32)
    earlier = (pos[None, :] < pos[:, None]).astype(jnp.bfloat16)
    before = jnp.dot(earlier, onehot, preferred_element_type=jnp.float32)
    slot_rank = jnp.sum(before * onehot.astype(jnp.float32), axis=1).astype(jnp.int32)
    holder = flat_ids // local_experts
    holder_xhi = (holder // hi_stride) % 2
    group_pos = (my_group ^ holder_xhi) * group_half + (holder // (2 * hi_stride)) * hi_stride + (
        holder % hi_stride
    )
    slot_of_pair = (group_pos * local_experts + flat_ids % local_experts) * capacity + slot_rank

    slot_ids = jnp.arange(slot_count, dtype=jnp.int32)
    pair_hit = slot_of_pair[None, :] == slot_ids[:, None]
    token_hit = jnp.any(pair_hit.reshape(slot_count, tok_rows, topk_count), axis=2)
    dispatch = token_hit.astype(jnp.bfloat16)
    slot_weight = jnp.sum(jnp.where(pair_hit, flat_weights[None, :], 0.0), axis=1)

    send_shape = (owners, local_experts * capacity, model_width)
    send_tokens = jnp.dot(dispatch, tokens_in, preferred_element_type=jnp.float32).astype(
        jnp.bfloat16
    )
    send_grads = jnp.dot(dispatch, out_grad, preferred_element_type=jnp.float32)
    send_scaled = (slot_weight[:, None] * send_grads).astype(jnp.bfloat16)
    recv_tokens = lax.all_to_all(
        send_tokens.reshape(send_shape), ("xlo", "expert"),
        split_axis=0,
        concat_axis=0,
        tiled=True,
        axis_index_groups=groups,
    )
    recv_scaled = lax.all_to_all(
        send_scaled.reshape(send_shape), ("xlo", "expert"),
        split_axis=0,
        concat_axis=0,
        tiled=True,
        axis_index_groups=groups,
    )
    block_shape = (owners, local_experts, capacity, model_width)
    recv_tokens = recv_tokens.reshape(block_shape)
    recv_scaled = recv_scaled.reshape(block_shape)

    gate_pre = jnp.einsum("nemd,deh->nemh", recv_tokens, w_gate, preferred_element_type=jnp.float32)
    up_pre = jnp.einsum("nemd,deh->nemh", recv_tokens, w_up, preferred_element_type=jnp.float32)
    sigmoid_gate = jax.nn.sigmoid(gate_pre)
    active = gate_pre * sigmoid_gate
    hidden = (active * up_pre).astype(jnp.bfloat16)
    hidden_grad = jnp.einsum(
        "nemd,deh->nemh", recv_scaled, w_down, preferred_element_type=jnp.float32
    )
    prob_part = jnp.sum(hidden_grad * hidden.astype(jnp.float32), axis=3).astype(jnp.bfloat16)
    gate_grad = (
        hidden_grad * up_pre * sigmoid_gate * (1.0 + gate_pre * (1.0 - sigmoid_gate))
    ).astype(jnp.bfloat16)
    up_grad = (hidden_grad * active).astype(jnp.bfloat16)
    block_count = xlo_count * core_count
    block_rows = model_width // block_count
    starts = [
        ((xlo ^ xlo_side) * core_count + (core ^ core_side)) * block_rows
        for xlo_side, core_side in ((1, 1), (0, 1), (1, 0), (0, 0))
    ]

    def blocks_of(left, right):
        blocks = [
            jnp.einsum(
                "nemh,nemd->ehd",
                left,
                lax.dynamic_slice_in_dim(right, at, block_rows, 3),
                preferred_element_type=jnp.float32,
            ).astype(jnp.bfloat16)
            for at in starts
        ]
        return jnp.stack(blocks[:2]), jnp.stack(blocks[2:])

    core_pairs = [(i, (i + 1) % core_count) for i in range(core_count)]
    xlo_pairs = [(i, (i + 1) % xlo_count) for i in range(xlo_count)]
    def core_sum(sib, own):
        from_sibling = lax.ppermute(sib, "core", core_pairs)
        return (own.astype(jnp.float32) + from_sibling.astype(jnp.float32)).astype(jnp.bfloat16)

    gate_sum, up_grad, hidden = lax.optimization_barrier(
        (core_sum(*blocks_of(gate_grad, recv_tokens)), up_grad, hidden)
    )
    up_sum, hidden = lax.optimization_barrier((core_sum(*blocks_of(up_grad, recv_tokens)), hidden))
    down_sib, down_own, gate_grad, up_grad = lax.optimization_barrier(
        blocks_of(hidden, recv_scaled) + (gate_grad, up_grad)
    )
    down_sum = core_sum(down_sib, down_own)

    shares = jnp.zeros((block_rows, 3, local_experts, hidden_width), jnp.bfloat16)
    for kind, summed in enumerate((gate_sum, up_sum, down_sum)):
        theirs = lax.ppermute(summed[0], "xlo", xlo_pairs)
        share = (summed[1].astype(jnp.float32) + theirs.astype(jnp.float32)).astype(jnp.bfloat16)
        shares = lax.dynamic_update_index_in_dim(shares, jnp.transpose(share, (2, 0, 1)), kind, 1)

    row_grad = (
        jnp.einsum("nemh,deh->nemd", gate_grad, w_gate, preferred_element_type=jnp.float32)
        + jnp.einsum("nemh,deh->nemd", up_grad, w_up, preferred_element_type=jnp.float32)
    ).astype(jnp.bfloat16)
    lane_pad = 128
    prob_cols = jnp.pad(prob_part[..., None], ((0, 0),) * 3 + ((0, lane_pad - 1),))
    back = lax.all_to_all(
        jnp.concatenate([row_grad, prob_cols], axis=3).reshape(
            owners, local_experts * capacity, model_width + lane_pad
        ),
        ("xlo", "expert"),
        split_axis=0,
        concat_axis=0,
        tiled=True,
        axis_index_groups=groups,
    ).reshape(slot_count, model_width + lane_pad)
    back_rows = back[:, :model_width]
    back_probs = back[:, model_width]

    input_grad = lax.dot_general(
        dispatch, back_rows, (((0,), (0,)), ((), ())), preferred_element_type=jnp.float32
    ).astype(jnp.bfloat16)
    pair_probs = jnp.sum(
        jnp.where(pair_hit, back_probs.astype(jnp.float32)[:, None], 0.0), axis=0
    ).reshape(tok_rows, topk_count)
    router_grad = pair_probs - weights * jnp.sum(pair_probs, axis=1, keepdims=True)

    return (input_grad, router_grad, shares)


def solution(mesh):
    dp_count, expert_devs = mesh.devices.shape
    core_count = 2
    split_mesh = Mesh(
        mesh.devices.reshape(dp_count // core_count, core_count, expert_devs),
        ("xlo", "core", "expert"),
    )
    rows = ("xlo", "core", "expert")
    in_specs = (
        P(rows, None),
        P(rows, None),
        P(rows, None),
        P(rows, None),
        P(None, "expert", None),
        P(None, "expert", None),
        P(None, "expert", None),
    )
    out_specs = (
        P(rows, None),
        P(rows, None),
        P(("xlo", "core"), None, "expert", None),
    )
    return jax.shard_map(
        per_device, mesh=split_mesh, in_specs=in_specs, out_specs=out_specs, check_vma=False
    )
```

```python
import jax
import jax.numpy as jnp
from jax import lax
from jax.sharding import Mesh
from jax.sharding import PartitionSpec as P


def combine_weights(gate_logits):
    raised = jnp.exp(gate_logits)
    return raised / jnp.sum(raised, axis=1, keepdims=True)


def diagonal_groups(xlo_count, owners, hi_stride):
    groups = [[], []]
    for xlo in range(xlo_count):
        for holder in range(owners):
            groups[xlo ^ ((holder // hi_stride) % 2)].append(xlo * owners + holder)
    return groups


def per_device(tokens_in, out_grad, gate_logits, route_ids, w_gate, w_up, w_down):
    tok_rows, model_width = tokens_in.shape
    topk_count = route_ids.shape[1]
    local_experts = w_gate.shape[1]
    hidden_width = w_gate.shape[2]
    xlo_count = lax.axis_size("xlo")
    core_count = lax.axis_size("core")
    owners = lax.axis_size("expert")
    expert_count = local_experts * owners
    capacity = 9 * tok_rows * topk_count // (8 * expert_count)
    pair_count = tok_rows * topk_count
    slot_count = expert_count * capacity
    xlo = lax.axis_index("xlo")
    core = lax.axis_index("core")
    hi_stride = 4
    group_half = owners // 2
    my_xhi = (lax.axis_index("expert") // hi_stride) % 2
    my_group = xlo ^ my_xhi
    groups = diagonal_groups(xlo_count, owners, hi_stride)

    weights = combine_weights(gate_logits)
    flat_ids = route_ids.reshape(-1)
    flat_weights = weights.reshape(-1)

    onehot = (flat_ids[:, None] == jnp.arange(expert_count, dtype=jnp.int32)[None, :]).astype(
        jnp.bfloat16
    )
    pos = jnp.arange(pair_count, dtype=jnp.int32)
    earlier = (pos[None, :] < pos[:, None]).astype(jnp.bfloat16)
    before = jnp.dot(earlier, onehot, preferred_element_type=jnp.float32)
    slot_rank = jnp.sum(before * onehot.astype(jnp.float32), axis=1).astype(jnp.int32)
    holder = flat_ids // local_experts
    holder_xhi = (holder // hi_stride) % 2
    group_pos = (my_group ^ holder_xhi) * group_half + (holder // (2 * hi_stride)) * hi_stride + (
        holder % hi_stride
    )
    slot_of_pair = (group_pos * local_experts + flat_ids % local_experts) * capacity + slot_rank

    slot_ids = jnp.arange(slot_count, dtype=jnp.int32)
    pair_hit = slot_of_pair[None, :] == slot_ids[:, None]
    token_hit = jnp.any(pair_hit.reshape(slot_count, tok_rows, topk_count), axis=2)
    dispatch = token_hit.astype(jnp.bfloat16)
    slot_weight = jnp.sum(jnp.where(pair_hit, flat_weights[None, :], 0.0), axis=1)

    send_shape = (owners, local_experts * capacity, model_width)
    picks = dispatch.reshape(owners, local_experts * capacity, tok_rows)
    send_tokens = jnp.einsum(
        "nst,td->nsd", picks, tokens_in, preferred_element_type=jnp.float32
    ).astype(jnp.bfloat16)
    send_grads = jnp.einsum("nst,td->nsd", picks, out_grad, preferred_element_type=jnp.float32)
    send_scaled = (
        slot_weight.reshape(owners, local_experts * capacity, 1) * send_grads
    ).astype(jnp.bfloat16)
    recv_tokens = lax.all_to_all(
        send_tokens.reshape(send_shape), ("xlo", "expert"),
        split_axis=0,
        concat_axis=0,
        tiled=True,
        axis_index_groups=groups,
    )
    recv_scaled = lax.all_to_all(
        send_scaled.reshape(send_shape), ("xlo", "expert"),
        split_axis=0,
        concat_axis=0,
        tiled=True,
        axis_index_groups=groups,
    )
    block_shape = (owners, local_experts, capacity, model_width)
    recv_tokens = recv_tokens.reshape(block_shape)
    recv_scaled = recv_scaled.reshape(block_shape)

    gate_pre = jnp.einsum("nemd,deh->nemh", recv_tokens, w_gate, preferred_element_type=jnp.float32)
    up_pre = jnp.einsum("nemd,deh->nemh", recv_tokens, w_up, preferred_element_type=jnp.float32)
    sigmoid_gate = jax.nn.sigmoid(gate_pre)
    active = gate_pre * sigmoid_gate
    hidden = (active * up_pre).astype(jnp.bfloat16)
    hidden_grad = jnp.einsum(
        "nemd,deh->nemh", recv_scaled, w_down, preferred_element_type=jnp.float32
    )
    prob_part = jnp.sum(hidden_grad * hidden.astype(jnp.float32), axis=3).astype(jnp.bfloat16)
    gate_grad = (
        hidden_grad * up_pre * sigmoid_gate * (1.0 + gate_pre * (1.0 - sigmoid_gate))
    ).astype(jnp.bfloat16)
    up_grad = (hidden_grad * active).astype(jnp.bfloat16)
    block_count = xlo_count * core_count
    block_rows = model_width // block_count
    starts = [
        ((xlo ^ xlo_side) * core_count + (core ^ core_side)) * block_rows
        for xlo_side, core_side in ((1, 1), (0, 1), (1, 0), (0, 0))
    ]

    def blocks_of(left, right):
        blocks = [
            jnp.einsum(
                "nemh,nemd->ehd",
                left,
                lax.dynamic_slice_in_dim(right, at, block_rows, 3),
                preferred_element_type=jnp.float32,
            ).astype(jnp.bfloat16)
            for at in starts
        ]
        return jnp.stack(blocks[:2]), jnp.stack(blocks[2:])

    core_pairs = [(i, (i + 1) % core_count) for i in range(core_count)]
    xlo_pairs = [(i, (i + 1) % xlo_count) for i in range(xlo_count)]
    gate_sib, gate_own = blocks_of(gate_grad, recv_tokens)
    gate_from, up_grad, hidden = lax.optimization_barrier(
        (lax.ppermute(gate_sib, "core", core_pairs), up_grad, hidden)
    )
    up_sib, up_own = blocks_of(up_grad, recv_tokens)
    up_from, hidden = lax.optimization_barrier((lax.ppermute(up_sib, "core", core_pairs), hidden))
    down_sib, down_own, gate_grad, up_grad = lax.optimization_barrier(
        blocks_of(hidden, recv_scaled) + (gate_grad, up_grad)
    )
    down_from = lax.ppermute(down_sib, "core", core_pairs)

    shares = jnp.zeros((block_rows, 3, local_experts, hidden_width), jnp.bfloat16)
    pieces = ((gate_from, gate_own), (up_from, up_own), (down_from, down_own))
    for kind, (from_sibling, own) in enumerate(pieces):
        summed = (own.astype(jnp.float32) + from_sibling.astype(jnp.float32)).astype(jnp.bfloat16)
        theirs = lax.ppermute(summed[0], "xlo", xlo_pairs)
        share = (summed[1].astype(jnp.float32) + theirs.astype(jnp.float32)).astype(jnp.bfloat16)
        shares = lax.dynamic_update_index_in_dim(shares, jnp.transpose(share, (2, 0, 1)), kind, 1)

    row_grad = (
        jnp.einsum("nemh,deh->nemd", gate_grad, w_gate, preferred_element_type=jnp.float32)
        + jnp.einsum("nemh,deh->nemd", up_grad, w_up, preferred_element_type=jnp.float32)
    ).astype(jnp.bfloat16)
    lane_pad = 128
    prob_cols = jnp.pad(prob_part[..., None], ((0, 0),) * 3 + ((0, lane_pad - 1),))
    back = lax.all_to_all(
        jnp.concatenate([row_grad, prob_cols], axis=3).reshape(
            owners, local_experts * capacity, model_width + lane_pad
        ),
        ("xlo", "expert"),
        split_axis=0,
        concat_axis=0,
        tiled=True,
        axis_index_groups=groups,
    ).reshape(slot_count, model_width + lane_pad)
    back_rows = back[:, :model_width]
    back_probs = back[:, model_width]

    input_grad = lax.dot_general(
        dispatch, back_rows, (((0,), (0,)), ((), ())), preferred_element_type=jnp.float32
    ).astype(jnp.bfloat16)
    pair_probs = jnp.sum(
        jnp.where(pair_hit, back_probs.astype(jnp.float32)[:, None], 0.0), axis=0
    ).reshape(tok_rows, topk_count)
    router_grad = pair_probs - weights * jnp.sum(pair_probs, axis=1, keepdims=True)

    return (input_grad, router_grad, shares)


def solution(mesh):
    dp_count, expert_devs = mesh.devices.shape
    core_count = 2
    split_mesh = Mesh(
        mesh.devices.reshape(dp_count // core_count, core_count, expert_devs),
        ("xlo", "core", "expert"),
    )
    rows = ("xlo", "core", "expert")
    in_specs = (
        P(rows, None),
        P(rows, None),
        P(rows, None),
        P(rows, None),
        P(None, "expert", None),
        P(None, "expert", None),
        P(None, "expert", None),
    )
    out_specs = (
        P(rows, None),
        P(rows, None),
        P(("xlo", "core"), None, "expert", None),
    )
    return jax.shard_map(
        per_device, mesh=split_mesh, in_specs=in_specs, out_specs=out_specs, check_vma=False
    )
```

```python
import jax
import jax.numpy as jnp
from jax import lax
from jax.sharding import Mesh
from jax.sharding import PartitionSpec as P


def combine_weights(gate_logits):
    raised = jnp.exp(gate_logits)
    return raised / jnp.sum(raised, axis=1, keepdims=True)


def diagonal_groups(xlo_count, owners, hi_stride):
    groups = [[], []]
    for xlo in range(xlo_count):
        for holder in range(owners):
            groups[xlo ^ ((holder // hi_stride) % 2)].append(xlo * owners + holder)
    return groups


def per_device(tokens_in, out_grad, gate_logits, route_ids, w_gate, w_up, w_down):
    tok_rows, model_width = tokens_in.shape
    topk_count = route_ids.shape[1]
    local_experts = w_gate.shape[1]
    hidden_width = w_gate.shape[2]
    xlo_count = lax.axis_size("xlo")
    core_count = lax.axis_size("core")
    owners = lax.axis_size("expert")
    expert_count = local_experts * owners
    capacity = 9 * tok_rows * topk_count // (8 * expert_count)
    pair_count = tok_rows * topk_count
    slot_count = expert_count * capacity
    xlo = lax.axis_index("xlo")
    core = lax.axis_index("core")
    hi_stride = 4
    group_half = owners // 2
    my_xhi = (lax.axis_index("expert") // hi_stride) % 2
    my_group = xlo ^ my_xhi
    groups = diagonal_groups(xlo_count, owners, hi_stride)

    weights = combine_weights(gate_logits)
    flat_ids = route_ids.reshape(-1)
    flat_weights = weights.reshape(-1)

    onehot = (flat_ids[:, None] == jnp.arange(expert_count, dtype=jnp.int32)[None, :]).astype(
        jnp.bfloat16
    )
    pos = jnp.arange(pair_count, dtype=jnp.int32)
    earlier = (pos[None, :] < pos[:, None]).astype(jnp.bfloat16)
    before = jnp.dot(earlier, onehot, preferred_element_type=jnp.float32)
    slot_rank = jnp.sum(before * onehot.astype(jnp.float32), axis=1).astype(jnp.int32)
    holder = flat_ids // local_experts
    holder_xhi = (holder // hi_stride) % 2
    group_pos = (my_group ^ holder_xhi) * group_half + (holder // (2 * hi_stride)) * hi_stride + (
        holder % hi_stride
    )
    slot_of_pair = (group_pos * local_experts + flat_ids % local_experts) * capacity + slot_rank

    slot_ids = jnp.arange(slot_count, dtype=jnp.int32)
    pair_hit = slot_of_pair[None, :] == slot_ids[:, None]
    token_hit = jnp.any(pair_hit.reshape(slot_count, tok_rows, topk_count), axis=2)
    dispatch = token_hit.astype(jnp.bfloat16)
    slot_weight = jnp.sum(jnp.where(pair_hit, flat_weights[None, :], 0.0), axis=1)

    send_shape = (owners, local_experts * capacity, model_width)
    picks = dispatch.reshape(owners, local_experts * capacity, tok_rows)
    send_tokens = jnp.einsum(
        "nst,td->nsd", picks, tokens_in, preferred_element_type=jnp.float32
    ).astype(jnp.bfloat16)
    send_grads = jnp.einsum("nst,td->nsd", picks, out_grad, preferred_element_type=jnp.float32)
    send_scaled = (
        slot_weight.reshape(owners, local_experts * capacity, 1) * send_grads
    ).astype(jnp.bfloat16)
    recv_tokens = lax.all_to_all(
        send_tokens.reshape(send_shape), ("xlo", "expert"),
        split_axis=0,
        concat_axis=0,
        tiled=True,
        axis_index_groups=groups,
    )
    recv_scaled = lax.all_to_all(
        send_scaled.reshape(send_shape), ("xlo", "expert"),
        split_axis=0,
        concat_axis=0,
        tiled=True,
        axis_index_groups=groups,
    )
    block_shape = (owners, local_experts, capacity, model_width)
    recv_tokens = recv_tokens.reshape(block_shape)
    recv_scaled = recv_scaled.reshape(block_shape)

    gate_pre = jnp.einsum("nemd,deh->nemh", recv_tokens, w_gate, preferred_element_type=jnp.float32)
    up_pre = jnp.einsum("nemd,deh->nemh", recv_tokens, w_up, preferred_element_type=jnp.float32)
    sigmoid_gate = jax.nn.sigmoid(gate_pre)
    active = gate_pre * sigmoid_gate
    hidden = (active * up_pre).astype(jnp.bfloat16)
    hidden_grad = jnp.einsum(
        "nemd,deh->nemh", recv_scaled, w_down, preferred_element_type=jnp.float32
    )
    prob_part = jnp.sum(hidden_grad * hidden.astype(jnp.float32), axis=3).astype(jnp.bfloat16)
    gate_grad = (
        hidden_grad * up_pre * sigmoid_gate * (1.0 + gate_pre * (1.0 - sigmoid_gate))
    ).astype(jnp.bfloat16)
    up_grad = (hidden_grad * active).astype(jnp.bfloat16)
    block_count = xlo_count * core_count
    block_rows = model_width // block_count
    starts = [
        ((xlo ^ xlo_side) * core_count + (core ^ core_side)) * block_rows
        for xlo_side, core_side in ((1, 1), (0, 1), (1, 0), (0, 0))
    ]

    def blocks_of(left, right):
        blocks = [
            jnp.einsum(
                "nemh,nemd->ehd",
                left,
                lax.dynamic_slice_in_dim(right, at, block_rows, 3),
                preferred_element_type=jnp.float32,
            ).astype(jnp.bfloat16)
            for at in starts
        ]
        return jnp.stack(blocks[:2]), jnp.stack(blocks[2:])

    core_pairs = [(i, (i + 1) % core_count) for i in range(core_count)]
    xlo_pairs = [(i, (i + 1) % xlo_count) for i in range(xlo_count)]
    gate_sib, gate_own = blocks_of(gate_grad, recv_tokens)
    gate_from, up_grad, hidden = lax.optimization_barrier(
        (lax.ppermute(gate_sib, "core", core_pairs), up_grad, hidden)
    )
    up_sib, up_own = blocks_of(up_grad, recv_tokens)
    up_from, hidden = lax.optimization_barrier((lax.ppermute(up_sib, "core", core_pairs), hidden))
    down_sib, down_own, gate_grad, up_grad = lax.optimization_barrier(
        blocks_of(hidden, recv_scaled) + (gate_grad, up_grad)
    )
    down_from = lax.ppermute(down_sib, "core", core_pairs)

    shares = jnp.zeros((block_rows, 3, local_experts, hidden_width), jnp.bfloat16)
    pieces = ((gate_from, gate_own), (up_from, up_own), (down_from, down_own))
    for kind, (from_sibling, own) in enumerate(pieces):
        summed = (own.astype(jnp.float32) + from_sibling.astype(jnp.float32)).astype(jnp.bfloat16)
        theirs = lax.ppermute(summed[0], "xlo", xlo_pairs)
        share = (summed[1].astype(jnp.float32) + theirs.astype(jnp.float32)).astype(jnp.bfloat16)
        shares = lax.dynamic_update_index_in_dim(shares, jnp.transpose(share, (2, 0, 1)), kind, 1)

    row_grad = (
        jnp.einsum("nemh,deh->nemd", gate_grad, w_gate, preferred_element_type=jnp.float32)
        + jnp.einsum("nemh,deh->nemd", up_grad, w_up, preferred_element_type=jnp.float32)
    ).astype(jnp.bfloat16)
    lane_pad = 128
    prob_cols = jnp.pad(prob_part[..., None], ((0, 0),) * 3 + ((0, lane_pad - 1),))
    back = lax.all_to_all(
        jnp.concatenate([row_grad, prob_cols], axis=3).reshape(
            owners, local_experts * capacity, model_width + lane_pad
        ),
        ("xlo", "expert"),
        split_axis=0,
        concat_axis=0,
        tiled=True,
        axis_index_groups=groups,
    )
    input_grad = jnp.einsum(
        "nst,nsd->td", picks, back[..., :model_width], preferred_element_type=jnp.float32
    ).astype(jnp.bfloat16)
    pair_probs = jnp.sum(
        jnp.where(
            pair_hit.reshape(owners, local_experts * capacity, pair_count),
            back[..., model_width].astype(jnp.float32)[..., None],
            0.0,
        ),
        axis=(0, 1),
    ).reshape(tok_rows, topk_count)
    router_grad = pair_probs - weights * jnp.sum(pair_probs, axis=1, keepdims=True)

    return (input_grad, router_grad, shares)


def solution(mesh):
    dp_count, expert_devs = mesh.devices.shape
    core_count = 2
    split_mesh = Mesh(
        mesh.devices.reshape(dp_count // core_count, core_count, expert_devs),
        ("xlo", "core", "expert"),
    )
    rows = ("xlo", "core", "expert")
    in_specs = (
        P(rows, None),
        P(rows, None),
        P(rows, None),
        P(rows, None),
        P(None, "expert", None),
        P(None, "expert", None),
        P(None, "expert", None),
    )
    out_specs = (
        P(rows, None),
        P(rows, None),
        P(("xlo", "core"), None, "expert", None),
    )
    return jax.shard_map(
        per_device, mesh=split_mesh, in_specs=in_specs, out_specs=out_specs, check_vma=False
    )
```

```python
import jax
import jax.numpy as jnp
from jax import lax
from jax.experimental.layout import Layout, with_layout_constraint
from jax.sharding import Mesh
from jax.sharding import PartitionSpec as P


def combine_weights(gate_logits):
    raised = jnp.exp(gate_logits)
    return raised / jnp.sum(raised, axis=1, keepdims=True)


def diagonal_groups(xlo_count, owners, hi_stride):
    groups = [[], []]
    for xlo in range(xlo_count):
        for holder in range(owners):
            groups[xlo ^ ((holder // hi_stride) % 2)].append(xlo * owners + holder)
    return groups


def per_device(tokens_in, out_grad, gate_logits, route_ids, w_gate, w_up, w_down):
    tok_rows, model_width = tokens_in.shape
    topk_count = route_ids.shape[1]
    local_experts = w_gate.shape[1]
    hidden_width = w_gate.shape[2]
    xlo_count = lax.axis_size("xlo")
    core_count = lax.axis_size("core")
    owners = lax.axis_size("expert")
    expert_count = local_experts * owners
    capacity = 9 * tok_rows * topk_count // (8 * expert_count)
    pair_count = tok_rows * topk_count
    slot_count = expert_count * capacity
    xlo = lax.axis_index("xlo")
    core = lax.axis_index("core")
    hi_stride = 4
    group_half = owners // 2
    my_xhi = (lax.axis_index("expert") // hi_stride) % 2
    my_group = xlo ^ my_xhi
    groups = diagonal_groups(xlo_count, owners, hi_stride)

    weights = combine_weights(gate_logits)
    flat_ids = route_ids.reshape(-1)
    flat_weights = weights.reshape(-1)

    onehot = (flat_ids[:, None] == jnp.arange(expert_count, dtype=jnp.int32)[None, :]).astype(
        jnp.bfloat16
    )
    pos = jnp.arange(pair_count, dtype=jnp.int32)
    earlier = (pos[None, :] < pos[:, None]).astype(jnp.bfloat16)
    before = jnp.dot(earlier, onehot, preferred_element_type=jnp.float32)
    slot_rank = jnp.sum(before * onehot.astype(jnp.float32), axis=1).astype(jnp.int32)
    holder = flat_ids // local_experts
    holder_xhi = (holder // hi_stride) % 2
    group_pos = (my_group ^ holder_xhi) * group_half + (holder // (2 * hi_stride)) * hi_stride + (
        holder % hi_stride
    )
    slot_of_pair = (group_pos * local_experts + flat_ids % local_experts) * capacity + slot_rank

    slot_ids = jnp.arange(slot_count, dtype=jnp.int32)
    pair_hit = slot_of_pair[None, :] == slot_ids[:, None]
    token_hit = jnp.any(pair_hit.reshape(slot_count, tok_rows, topk_count), axis=2)
    dispatch = token_hit.astype(jnp.bfloat16)
    slot_weight = jnp.sum(jnp.where(pair_hit, flat_weights[None, :], 0.0), axis=1)

    send_shape = (owners, local_experts * capacity, model_width)
    picks = dispatch.reshape(owners, local_experts * capacity, tok_rows)
    send_tokens = jnp.einsum(
        "nst,td->nsd", picks, tokens_in, preferred_element_type=jnp.float32
    ).astype(jnp.bfloat16)
    send_grads = jnp.einsum("nst,td->nsd", picks, out_grad, preferred_element_type=jnp.float32)
    send_scaled = (
        slot_weight.reshape(owners, local_experts * capacity, 1) * send_grads
    ).astype(jnp.bfloat16)
    recv_tokens = lax.all_to_all(
        send_tokens.reshape(send_shape), ("xlo", "expert"),
        split_axis=0,
        concat_axis=0,
        tiled=True,
        axis_index_groups=groups,
    )
    recv_scaled = lax.all_to_all(
        send_scaled.reshape(send_shape), ("xlo", "expert"),
        split_axis=0,
        concat_axis=0,
        tiled=True,
        axis_index_groups=groups,
    )
    block_shape = (owners, local_experts, capacity, model_width)
    recv_tokens = recv_tokens.reshape(block_shape)
    recv_scaled = recv_scaled.reshape(block_shape)

    gate_pre = jnp.einsum("nemd,deh->nemh", recv_tokens, w_gate, preferred_element_type=jnp.float32)
    up_pre = jnp.einsum("nemd,deh->nemh", recv_tokens, w_up, preferred_element_type=jnp.float32)
    sigmoid_gate = jax.nn.sigmoid(gate_pre)
    active = gate_pre * sigmoid_gate
    hidden = (active * up_pre).astype(jnp.bfloat16)
    hidden_grad = jnp.einsum(
        "nemd,deh->nemh", recv_scaled, w_down, preferred_element_type=jnp.float32
    )
    prob_part = jnp.sum(hidden_grad * hidden.astype(jnp.float32), axis=3).astype(jnp.bfloat16)
    gate_grad = (
        hidden_grad * up_pre * sigmoid_gate * (1.0 + gate_pre * (1.0 - sigmoid_gate))
    ).astype(jnp.bfloat16)
    up_grad = (hidden_grad * active).astype(jnp.bfloat16)
    block_count = xlo_count * core_count
    block_rows = model_width // block_count
    starts = [
        ((xlo ^ xlo_side) * core_count + (core ^ core_side)) * block_rows
        for xlo_side, core_side in ((1, 1), (0, 1), (1, 0), (0, 0))
    ]

    def blocks_of(left, right):
        blocks = [
            jnp.einsum(
                "nemh,nemd->ehd",
                left,
                lax.dynamic_slice_in_dim(right, at, block_rows, 3),
                preferred_element_type=jnp.float32,
            ).astype(jnp.bfloat16)
            for at in starts
        ]
        return jnp.stack(blocks[:2]), jnp.stack(blocks[2:])

    core_pairs = [(i, (i + 1) % core_count) for i in range(core_count)]
    xlo_pairs = [(i, (i + 1) % xlo_count) for i in range(xlo_count)]
    gate_sib, gate_own = blocks_of(gate_grad, recv_tokens)
    gate_from, up_grad, hidden = lax.optimization_barrier(
        (lax.ppermute(gate_sib, "core", core_pairs), up_grad, hidden)
    )
    up_sib, up_own = blocks_of(up_grad, recv_tokens)
    up_from, hidden = lax.optimization_barrier((lax.ppermute(up_sib, "core", core_pairs), hidden))
    down_sib, down_own, gate_grad, up_grad = lax.optimization_barrier(
        blocks_of(hidden, recv_scaled) + (gate_grad, up_grad)
    )
    down_from = lax.ppermute(down_sib, "core", core_pairs)

    shares = jnp.zeros((block_rows, 3, local_experts, hidden_width), jnp.bfloat16)
    pieces = ((gate_from, gate_own), (up_from, up_own), (down_from, down_own))
    for kind, (from_sibling, own) in enumerate(pieces):
        summed = (own.astype(jnp.float32) + from_sibling.astype(jnp.float32)).astype(jnp.bfloat16)
        theirs = lax.ppermute(summed[0], "xlo", xlo_pairs)
        share = (summed[1].astype(jnp.float32) + theirs.astype(jnp.float32)).astype(jnp.bfloat16)
        shares = with_layout_constraint(
            lax.dynamic_update_index_in_dim(shares, jnp.transpose(share, (2, 0, 1)), kind, 1),
            Layout((0, 1, 2, 3)),
        )

    row_grad = (
        jnp.einsum("nemh,deh->nemd", gate_grad, w_gate, preferred_element_type=jnp.float32)
        + jnp.einsum("nemh,deh->nemd", up_grad, w_up, preferred_element_type=jnp.float32)
    ).astype(jnp.bfloat16)
    lane_pad = 128
    prob_cols = jnp.pad(prob_part[..., None], ((0, 0),) * 3 + ((0, lane_pad - 1),))
    back = lax.all_to_all(
        jnp.concatenate([row_grad, prob_cols], axis=3).reshape(
            owners, local_experts * capacity, model_width + lane_pad
        ),
        ("xlo", "expert"),
        split_axis=0,
        concat_axis=0,
        tiled=True,
        axis_index_groups=groups,
    )
    input_grad = jnp.einsum(
        "nst,nsd->td", picks, back[..., :model_width], preferred_element_type=jnp.float32
    ).astype(jnp.bfloat16)
    pair_probs = jnp.sum(
        jnp.where(
            pair_hit.reshape(owners, local_experts * capacity, pair_count),
            back[..., model_width].astype(jnp.float32)[..., None],
            0.0,
        ),
        axis=(0, 1),
    ).reshape(tok_rows, topk_count)
    router_grad = pair_probs - weights * jnp.sum(pair_probs, axis=1, keepdims=True)

    return (input_grad, router_grad, shares)


def solution(mesh):
    dp_count, expert_devs = mesh.devices.shape
    core_count = 2
    split_mesh = Mesh(
        mesh.devices.reshape(dp_count // core_count, core_count, expert_devs),
        ("xlo", "core", "expert"),
    )
    rows = ("xlo", "core", "expert")
    in_specs = (
        P(rows, None),
        P(rows, None),
        P(rows, None),
        P(rows, None),
        P(None, "expert", None),
        P(None, "expert", None),
        P(None, "expert", None),
    )
    out_specs = (
        P(rows, None),
        P(rows, None),
        P(("xlo", "core"), None, "expert", None),
    )
    return jax.shard_map(
        per_device, mesh=split_mesh, in_specs=in_specs, out_specs=out_specs, check_vma=False
    )
```
